256 devices in a mesh: tm: 32 (over y_hi, z, core), space: 8 (over y_lo, x).
Axes of the slice: x: 4, y: 4 (y_hi: 2, y_lo: 2; y = y_hi * 2 + y_lo), z: 8, core: 2. Of those that a mesh axis runs over, the one named last changes fastest.
Arguments:
- start_state: float32 [32, 64, 8192], P('tm', None, 'space'), may hold values from -1.2 to 1.2
- stiffness: float32 [64, 64], replicated, may hold values from -0.75 to 0.75
- lifting: float32 [64, 96], replicated, may hold values from -0.625 to 0.625
- coarse: float32 [64, 64], replicated
- neighbor: int32 [6, 8192], P(None, 'space'), may hold values from 0 to 2047, as said below
- orientation: int32 [6, 8192], P(None, 'space'), may hold values from 0 to 7
- send_low: int32 [4096], P('space'), may hold values from 0 to 1023, as said below
- send_high: int32 [4096], P('space'), may hold values from 0 to 1023, as said below
Outputs:
- end_state: float32 [32, 64, 8192], P('tm', None, 'space')
The draws below stay inside these ranges and needn't reach their ends.
Inputs may be any that keep to these rules, and one draw needn't show every extreme that they name: `send_low`: distinct local slots of one partition, 512 per partition; the lower boundary elements of a partition are the upper neighbours, across face 1, of the upper boundary elements of the partition below, in the same order. `send_high`: distinct local slots of one partition, 512 per partition. `neighbor`: values of 1024 or more occur only for face 0 (first 512 halo slots) and face 1 (next 512 halo slots); each halo slot is named by exactly one element.
All inputs are finite; a program needn't handle non-finite values.
Results may differ from the reference program's by a relative error of at most 0.00015.
Values sent between devices are 32-bit elements; how exact they have to be, the bound alone decides.
No kernel may reach another device: no remote copies, remote signals or barrier semaphores. Data moves between devices by JAX's collectives and lax.ppermute only.
A program may use at most 64 MiB of HBM per device.

```python
import jax
import jax.numpy as jnp
from jax import lax

NODES = 64
STEPS = 3
CXE = 2
EY = 16
EZ = 32
E_DEV = 1024
BND = 512
NE = 8192
SLICES = 32
N_SPACE = 8


def relabel(orders, device_ids, value, position):
    current = orders[:, position]
    swapped = jnp.where(orders == value, current[:, None], jnp.where(orders == current[:, None], value, orders))
    return jnp.where(device_ids[:, None], swapped, orders).astype(jnp.int32)


def layout(key):
    base_key = jax.random.fold_in(key, 11)
    orders = jax.vmap(lambda device_id: jax.random.permutation(jax.random.fold_in(base_key, device_id), E_DEV))(jnp.arange(N_SPACE))
    orders = orders.astype(jnp.int32)
    device_ids = jnp.arange(N_SPACE, dtype=jnp.int32)
    first_dev = device_ids == 0
    last_dev = device_ids == N_SPACE - 1
    orders = relabel(orders, first_dev, E_DEV - 1, 0)
    orders = relabel(orders, first_dev, 0, E_DEV - 1)
    orders = relabel(orders, last_dev, E_DEV - 1, E_DEV - 1)
    orders = relabel(orders, last_dev, 0, 0)
    cell_ids = jnp.arange(E_DEV, dtype=jnp.int32)
    plane = EY * EZ
    slab_layer = cell_ids // plane
    plane_row = cell_ids // EZ % EY
    plane_col = cell_ids % EZ
    bnd_index = plane_row * EZ + plane_col

    def cell_at(layer_id, row_id, col_id):
        return layer_id * plane + row_id * EZ + col_id
    face_low = jnp.where(slab_layer[None, :] > 0, orders[:, cell_at(jnp.maximum(slab_layer - 1, 0), plane_row, plane_col)], E_DEV + bnd_index[None, :])
    face_high = jnp.where(slab_layer[None, :] < CXE - 1, orders[:, cell_at(jnp.minimum(slab_layer + 1, CXE - 1), plane_row, plane_col)], E_DEV + BND + bnd_index[None, :])
    face_two = orders[:, cell_at(slab_layer, (plane_row - 1) % EY, plane_col)]
    face_three = orders[:, cell_at(slab_layer, (plane_row + 1) % EY, plane_col)]
    face_four = orders[:, cell_at(slab_layer, plane_row, (plane_col - 1) % EZ)]
    face_five = orders[:, cell_at(slab_layer, plane_row, (plane_col + 1) % EZ)]
    values = jnp.stack([face_low, face_high, face_two, face_three, face_four, face_five]).astype(jnp.int32)
    placed = jnp.zeros((6, N_SPACE, E_DEV), jnp.int32).at[:, jnp.arange(N_SPACE)[:, None], orders].set(values)
    return (placed.reshape(6, N_SPACE * E_DEV), orders[:, :BND].reshape(-1), orders[:, (CXE - 1) * BND:].reshape(-1))


def draw_neighbor(key, part):
    return layout(key)[0]


def draw_send_low(key, part):
    return layout(key)[1]


def draw_send_high(key, part):
    return layout(key)[2]


def draw_coarse(key, part):
    diag_key = jax.random.fold_in(key, 21)
    off_key = jax.random.fold_in(key, 22)
    diag_vals = jnp.exp(jax.random.uniform(diag_key, (NODES,), jnp.float32, jnp.log(0.6), jnp.log(0.85)))
    off_vals = 0.02 * jax.random.normal(off_key, (NODES, NODES), jnp.float32)
    identity = jnp.eye(NODES, dtype=jnp.float32)
    return off_vals * (1.0 - identity) + identity * diag_vals[None, :]


def set_ends(result, own_key, low, top_value):
    extent = result.shape
    place = [jax.random.randint(jax.random.fold_in(own_key, axis), (), 0, extent[axis]) for axis in range(len(extent))]
    result = result.at[tuple(place)].set(low)
    longest = extent.index(max(extent))
    place[longest] = (place[longest] + 1) % extent[longest]
    return result.at[tuple(place)].set(top_value)


def steps_of(own_key, shape, shards, low, largest):
    loudness, own = 1.0, jax.random.fold_in(own_key, 6)
    for axis_at, parts in shards:
        heights = jnp.exp(jax.random.uniform(jax.random.fold_in(own, axis_at), (parts,), jnp.float32, low / len(shards), largest / len(shards)))
        loudness = loudness * jnp.repeat(heights, shape[axis_at] // parts).reshape([-1 if axis == axis_at else 1 for axis in range(len(shape))])
    return loudness


def bell_draw(own_key, shape, scale, bound, kind=jnp.bfloat16):
    array = jax.random.normal(own_key, shape, jnp.float32) * scale
    return jnp.minimum(jnp.maximum(array, -bound), bound).astype(kind)


def setup_inputs(seed: int = 0) -> dict:
    splits = jax.random.split(jax.random.key(seed), 9)
    return {
        "start_state": jnp.clip(jax.random.uniform(splits[0], (SLICES, NODES, NE), jnp.float32, -1.2, 1.2) * steps_of(splits[0], (SLICES, NODES, NE), ((0, 32), (2, 8)), -0.4, 0.0), -1.2, 1.2),
        "stiffness": bell_draw(splits[1], (NODES, NODES), NODES ** -0.5, 0.75, jnp.float32),
        "lifting": bell_draw(splits[2], (NODES, 6 * 16), (6 * 16) ** -0.5, 0.625, jnp.float32),
        "coarse": draw_coarse(jax.random.fold_in(splits[8], 71), 0),
        "neighbor": draw_neighbor(jax.random.fold_in(splits[8], 71), 0),
        "orientation": set_ends(jax.random.randint(splits[5], (6, NE), 0, 8), jax.random.fold_in(splits[5], 1), 0, 7).astype(jnp.int32),
        "send_low": draw_send_low(jax.random.fold_in(splits[8], 71), 0),
        "send_high": draw_send_high(jax.random.fold_in(splits[8], 71), 0),
    }


time_step = 0.05


def product(matrix, vector):
    return jnp.dot(matrix, vector, precision=lax.Precision.HIGHEST, preferred_element_type=jnp.float32)


def face_traces(state_now):
    elements = state_now.shape[1]
    cube_view = state_now.reshape(4, 4, 4, elements)
    return [cube_view[0], cube_view[3], cube_view[:, 0], cube_view[:, 3], cube_view[:, :, 0], cube_view[:, :, 3]]


def oriented(trace, code_row):
    summed = jnp.zeros_like(trace)
    for variant in range(8):
        turned = trace
        if variant & 4:
            turned = jnp.swapaxes(turned, 0, 1)
        if variant & 1:
            turned = turned[::-1]
        if variant & 2:
            turned = turned[:, ::-1]
        summed = summed + jnp.where(code_row == variant, turned, 0.0)
    return summed


def tendency(state_now, own_list, near_list, stiffness, lifting, orientation):
    elements = state_now.shape[1]
    jump_list = []
    for face_id in range(6):
        jump_list.append((oriented(near_list[face_id], orientation[face_id]) - own_list[face_id]).reshape(16, elements))
    stacked = jnp.concatenate(jump_list, axis=0)
    return product(stiffness, state_now) + product(lifting, stacked) + state_now - state_now * state_now * state_now


def reference(start_state, stiffness, lifting, coarse, neighbor, orientation, send_low, send_high):
    total = E_DEV * N_SPACE
    device_of = jnp.arange(total, dtype=jnp.int32) // E_DEV
    lower_dev = (device_of - 1) % N_SPACE
    upper_dev = (device_of + 1) % N_SPACE
    low_index = jnp.clip(neighbor - E_DEV, 0, BND - 1).astype(jnp.int32)
    high_index = jnp.clip(neighbor - E_DEV - BND, 0, BND - 1).astype(jnp.int32)
    from_lower = lower_dev * E_DEV + send_high[lower_dev * BND + low_index]
    from_upper = upper_dev * E_DEV + send_low[upper_dev * BND + high_index]
    global_nb = jnp.where(neighbor < E_DEV, device_of * E_DEV + neighbor,
                          jnp.where(neighbor < E_DEV + BND, from_lower, from_upper)).astype(jnp.int32)

    def fine_slice(state_now):
        for step_id in range(STEPS):
            own_list = face_traces(state_now)
            near_list = []
            for face_id in range(6):
                source = own_list[face_id ^ 1].reshape(16, total)
                near_list.append(jnp.take(source, global_nb[face_id], axis=1).reshape(4, 4, total))
            state_now = state_now + time_step * tendency(state_now, own_list, near_list, stiffness, lifting, orientation)
        return state_now

    fine_all = lax.map(fine_slice, start_state)
    defect = fine_all - jax.vmap(lambda slice_state: product(coarse, slice_state))(start_state)

    def advance(carry_state, defect_now):
        end_now = product(coarse, carry_state) + defect_now
        return end_now, end_now

    last_state, ends = lax.scan(advance, start_state[0], defect)
    return ends
```

```python
import jax
import jax.numpy as jnp
from jax import lax
from jax.sharding import PartitionSpec as P

STEPS = 3


time_step = 0.05


def with_halo(shard, sides, width):
    for axis, dim in sides:
        peers, length = (lax.axis_size(axis), shard.shape[dim])
        up = [(i, (i + 1) % peers) for i in range(peers)]
        down = [(j, i) for i, j in up]
        last = lax.slice_in_dim(shard, length - width, length, axis=dim)
        initial = lax.slice_in_dim(shard, 0, width, axis=dim)
        before = lax.ppermute(last, axis, up)
        after = lax.ppermute(initial, axis, down)
        shard = jnp.concatenate([before, shard, after], axis=dim)
    return shard


def from_behind(shard, axis, by):
    peers = lax.axis_size(axis)
    pairs = [(i, i + by) for i in range(peers) if 0 <= i + by < peers]
    return lax.ppermute(shard, axis, pairs)


def product(matrix, vector):
    return jnp.dot(
        matrix, vector, precision=lax.Precision.HIGHEST, preferred_element_type=jnp.float32
    )


def face_traces(state_now):
    elements = state_now.shape[1]
    cube_view = state_now.reshape(4, 4, 4, elements)
    return [
        cube_view[0],
        cube_view[3],
        cube_view[:, 0],
        cube_view[:, 3],
        cube_view[:, :, 0],
        cube_view[:, :, 3],
    ]


def oriented_all(traces, codes):
    summed = jnp.zeros_like(traces)
    for variant in range(8):
        turned = traces
        if variant & 4:
            turned = jnp.swapaxes(turned, 1, 2)
        if variant & 1:
            turned = turned[:, ::-1]
        if variant & 2:
            turned = turned[:, :, ::-1]
        summed = summed + jnp.where(codes[:, None, None, :] == variant, turned, 0.0)
    return summed


def fine_step(state_now, stiffness, lifting, neighbor, orientation, send_low, send_high):
    elements = state_now.shape[1]
    own_list = face_traces(state_now)
    own_stack = jnp.stack(own_list)
    flat_stack = own_stack.reshape(6, 16, elements)
    outgoing = jnp.stack(
        [jnp.take(flat_stack[0], send_low, axis=1), jnp.take(flat_stack[1], send_high, axis=1)]
    )
    received = with_halo(outgoing, (("space", 0),), 1)
    opposite = flat_stack[jnp.array([1, 0, 3, 2, 5, 4])]
    halo_part = jnp.concatenate([received[0], received[3]], axis=1)
    bound = halo_part.shape[1]
    extended = jnp.concatenate(
        [opposite, jnp.broadcast_to(halo_part[None], (6, 16, bound))], axis=2
    )
    beside = jnp.take_along_axis(extended, neighbor[:, None, :], axis=2).reshape(6, 4, 4, elements)
    jumps = oriented_all(beside, orientation) - own_stack
    stacked = jumps.reshape(96, elements)
    rate = (
        product(stiffness, state_now)
        + product(lifting, stacked)
        + state_now
        - state_now * state_now * state_now
    )
    return state_now + time_step * rate


def shards(start_state, stiffness, lifting, coarse, neighbor, orientation, send_low, send_high):
    state_start = start_state[0]
    fine_state = state_start
    for step_id in range(STEPS):
        fine_state = fine_step(
            fine_state, stiffness, lifting, neighbor, orientation, send_low, send_high
        )
    coarse_start = product(coarse, state_start)
    defect = fine_state - coarse_start
    is_first = lax.axis_index("tm") == 0
    total = jnp.where(is_first, coarse_start + defect, defect)
    power = coarse
    offset = 1
    peers = lax.axis_size("tm")
    while offset < peers:
        arrived = from_behind(total, "tm", offset)
        total = total + product(power, arrived)
        offset *= 2
        if offset < peers:
            power = product(power, power)
    return total[None]


def solution(mesh):
    return jax.shard_map(
        shards,
        mesh=mesh,
        in_specs=(
            P("tm", None, "space"),
            P(),
            P(),
            P(),
            P(None, "space"),
            P(None, "space"),
            P("space"),
            P("space"),
        ),
        out_specs=P("tm", None, "space"),
        check_vma=False,
    )
```

```python
import functools

import numpy as np
import jax
import jax.numpy as jnp
from jax import lax
from jax.experimental import pallas as pl
from jax.experimental.pallas import tpu as pltpu
from jax.sharding import PartitionSpec as P

STEPS = 3
LANES = 128
UNROLL = 8


time_step = 0.05


def from_behind(shard, axis, by):
    peers = lax.axis_size(axis)
    pairs = [(i, i + by) for i in range(peers) if 0 <= i + by < peers]
    return lax.ppermute(shard, axis, pairs)


def ring(shard, axis, by):
    peers = lax.axis_size(axis)
    return lax.ppermute(shard, axis, [(i, (i + by) % peers) for i in range(peers)])


def product(matrix, vector):
    return jnp.dot(
        matrix, vector, precision=lax.Precision.HIGHEST, preferred_element_type=jnp.float32
    )


def face_nodes():
    i, j, k = np.meshgrid(np.arange(4), np.arange(4), np.arange(4), indexing="ij")
    node = 16 * i + 4 * j + k
    return [
        node[0].ravel(), node[3].ravel(),
        node[:, 0].ravel(), node[:, 3].ravel(),
        node[:, :, 0].ravel(), node[:, :, 3].ravel(),
    ]


def orientations():
    base = np.arange(16).reshape(4, 4)
    out = []
    for code in range(8):
        turned = base
        if code & 4:
            turned = turned.T
        if code & 1:
            turned = turned[::-1]
        if code & 2:
            turned = turned[:, ::-1]
        out.append(turned.ravel())
    return out


def selection_tables():
    nodes, perms = face_nodes(), orientations()
    pick = np.zeros((6, LANES, LANES), np.float32)
    own = np.zeros((64, 96), np.float32)
    for f in range(6):
        for code in range(8):
            for q in range(16):
                pick[f, nodes[f ^ 1][perms[code][q]], 16 * code + q] = 1.0
        for m in range(16):
            own[nodes[f][m], 16 * f + m] = 1.0
    return pick, own


def gather_kernel(idx_ref, table_ref, out_ref):
    def body(step, carry):
        for u in range(UNROLL):
            row = step * UNROLL + u
            out_ref[pl.ds(row, 1), :] = table_ref[pl.ds(idx_ref[row], 1), :]
        return carry

    lax.fori_loop(0, out_ref.shape[0] // UNROLL, body, 0)


def gather_rows(table, idx):
    return pl.pallas_call(
        gather_kernel,
        out_shape=jax.ShapeDtypeStruct((idx.shape[0], table.shape[1]), table.dtype),
        in_specs=[
            pl.BlockSpec(memory_space=pltpu.SMEM),
            pl.BlockSpec(memory_space=pltpu.VMEM),
        ],
        out_specs=pl.BlockSpec(memory_space=pltpu.VMEM),
    )(idx, table)


def fine_step(state, folded, pick, spread, mask, nbr_rows, send_rows):
    elements = state.shape[0]
    padded = jnp.pad(state, ((0, 0), (0, LANES - state.shape[1])))
    sent = gather_rows(padded, send_rows)
    half = sent.shape[0] // 2
    low_trace = sent[:half, 0:16].T
    high_trace = sent[half:, 48:64].T
    before = ring(high_trace, "space", 1)
    after = ring(low_trace, "space", -1)
    halo_low = jnp.pad(before.T, ((0, 0), (48, LANES - 64)))
    halo_high = jnp.pad(after.T, ((0, 0), (0, LANES - 16)))
    table = jnp.concatenate([padded, halo_low, halo_high], axis=0)
    beside = gather_rows(table, nbr_rows).reshape(6, elements, LANES)
    turned = jnp.einsum(
        "fer,frq->feq", beside, pick, precision=lax.Precision.HIGHEST,
        preferred_element_type=jnp.float32,
    )
    chosen = jnp.where(mask, turned, 0.0)
    lifted = jnp.einsum(
        "feq,fqn->en", chosen, spread, precision=lax.Precision.HIGHEST,
        preferred_element_type=jnp.float32,
    )
    rate = product(state, folded) + lifted + state - state * state * state
    return state + time_step * rate


def shards(start_state, stiffness, lifting, coarse, neighbor, orientation, send_low, send_high):
    pick_np, own_np = selection_tables()
    pick = jnp.asarray(pick_np)
    own = jnp.asarray(own_np)
    lift_t = lifting.T.reshape(6, 16, 64)
    spread = jnp.broadcast_to(lift_t[:, None], (6, 8, 16, 64)).reshape(6, LANES, 64)
    folded = stiffness.T - product(own, lifting.T)
    lane_code = jnp.arange(LANES, dtype=jnp.int32) // 16
    mask = orientation[:, :, None] == lane_code[None, None, :]
    nbr_rows = neighbor.reshape(-1)
    send_rows = jnp.concatenate([send_low, send_high])

    state_start = start_state[0]
    fine_state = state_start.T
    for step_id in range(STEPS):
        fine_state = fine_step(fine_state, folded, pick, spread, mask, nbr_rows, send_rows)
    fine_state = fine_state.T
    coarse_start = product(coarse, state_start)
    defect = fine_state - coarse_start
    is_first = lax.axis_index("tm") == 0
    total = jnp.where(is_first, coarse_start + defect, defect)
    power = coarse
    offset = 1
    peers = lax.axis_size("tm")
    while offset < peers:
        arrived = from_behind(total, "tm", offset)
        total = total + product(power, arrived)
        offset *= 2
        if offset < peers:
            power = product(power, power)
    return total[None]


def solution(mesh):
    return jax.shard_map(
        shards,
        mesh=mesh,
        in_specs=(
            P("tm", None, "space"),
            P(),
            P(),
            P(),
            P(None, "space"),
            P(None, "space"),
            P("space"),
            P("space"),
        ),
        out_specs=P("tm", None, "space"),
        check_vma=False,
    )
```

```python
import functools

import numpy as np
import jax
import jax.numpy as jnp
from jax import lax
from jax.experimental import pallas as pl
from jax.experimental.pallas import tpu as pltpu
from jax.sharding import PartitionSpec as P

STEPS = 3
LANES = 128
UNROLL = 8
SCAN_PIECES = 4


time_step = 0.05


def from_behind(shard, axis, by):
    peers = lax.axis_size(axis)
    pairs = [(i, i + by) for i in range(peers) if 0 <= i + by < peers]
    return lax.ppermute(shard, axis, pairs)


def ring(shard, axis, by):
    peers = lax.axis_size(axis)
    return lax.ppermute(shard, axis, [(i, (i + by) % peers) for i in range(peers)])


def product(matrix, vector):
    return jnp.dot(
        matrix, vector, precision=lax.Precision.HIGHEST, preferred_element_type=jnp.float32
    )


def face_nodes():
    i, j, k = np.meshgrid(np.arange(4), np.arange(4), np.arange(4), indexing="ij")
    node = 16 * i + 4 * j + k
    return [
        node[0].ravel(), node[3].ravel(),
        node[:, 0].ravel(), node[:, 3].ravel(),
        node[:, :, 0].ravel(), node[:, :, 3].ravel(),
    ]


def orientations():
    base = np.arange(16).reshape(4, 4)
    out = []
    for code in range(8):
        turned = base
        if code & 4:
            turned = turned.T
        if code & 1:
            turned = turned[::-1]
        if code & 2:
            turned = turned[:, ::-1]
        out.append(turned.ravel())
    return out


def selection_tables():
    nodes, perms = face_nodes(), orientations()
    pick = np.zeros((6, LANES, LANES), np.float32)
    own = np.zeros((64, 96), np.float32)
    for f in range(6):
        for code in range(8):
            for q in range(16):
                pick[f, nodes[f ^ 1][perms[code][q]], 16 * code + q] = 1.0
        for m in range(16):
            own[nodes[f][m], 16 * f + m] = 1.0
    return pick, own


def gather_kernel(idx_ref, table_ref, out_ref):
    def body(step, carry):
        for u in range(UNROLL):
            row = step * UNROLL + u
            out_ref[pl.ds(row, 1), :] = table_ref[pl.ds(idx_ref[row], 1), :]
        return carry

    lax.fori_loop(0, out_ref.shape[0] // UNROLL, body, 0)


def gather_rows(table, idx):
    return pl.pallas_call(
        gather_kernel,
        out_shape=jax.ShapeDtypeStruct((idx.shape[0], table.shape[1]), table.dtype),
        in_specs=[
            pl.BlockSpec(memory_space=pltpu.SMEM),
            pl.BlockSpec(memory_space=pltpu.VMEM),
        ],
        out_specs=pl.BlockSpec(memory_space=pltpu.VMEM),
    )(idx, table)


def fine_step(state, folded, pick, spread, mask, nbr_rows, send_rows):
    elements = state.shape[0]
    padded = jnp.pad(state, ((0, 0), (0, LANES - state.shape[1])))
    sent = gather_rows(padded, send_rows)
    half = sent.shape[0] // 2
    low_trace = sent[:half, 0:16].T
    high_trace = sent[half:, 48:64].T
    before = ring(high_trace, "space", 1)
    after = ring(low_trace, "space", -1)
    halo_low = jnp.pad(before.T, ((0, 0), (48, LANES - 64)))
    halo_high = jnp.pad(after.T, ((0, 0), (0, LANES - 16)))
    table = jnp.concatenate([padded, halo_low, halo_high], axis=0)
    beside = gather_rows(table, nbr_rows).reshape(6, elements, LANES)
    turned = jnp.einsum(
        "fer,frq->feq", beside, pick, precision=lax.Precision.HIGHEST,
        preferred_element_type=jnp.float32,
    )
    chosen = jnp.where(mask, turned, 0.0)
    lifted = jnp.einsum(
        "feq,fqn->en", chosen, spread, precision=lax.Precision.HIGHEST,
        preferred_element_type=jnp.float32,
    )
    rate = product(state, folded) + lifted + state - state * state * state
    return state + time_step * rate


def shards(start_state, stiffness, lifting, coarse, neighbor, orientation, send_low, send_high):
    pick_np, own_np = selection_tables()
    pick = jnp.asarray(pick_np)
    own = jnp.asarray(own_np)
    lift_t = lifting.T.reshape(6, 16, 64)
    spread = jnp.broadcast_to(lift_t[:, None], (6, 8, 16, 64)).reshape(6, LANES, 64)
    folded = stiffness.T - product(own, lifting.T)
    lane_code = jnp.arange(LANES, dtype=jnp.int32) // 16
    mask = orientation[:, :, None] == lane_code[None, None, :]
    nbr_rows = neighbor.reshape(-1)
    send_rows = jnp.concatenate([send_low, send_high])

    state_start = start_state[0]
    fine_state = state_start.T
    for step_id in range(STEPS):
        fine_state = fine_step(fine_state, folded, pick, spread, mask, nbr_rows, send_rows)
    fine_state = fine_state.T
    coarse_start = product(coarse, state_start)
    defect = fine_state - coarse_start
    is_first = lax.axis_index("tm") == 0
    total = jnp.where(is_first, coarse_start + defect, defect)
    power = coarse
    offset = 1
    peers = lax.axis_size("tm")
    while offset < peers:
        pieces = jnp.split(total, SCAN_PIECES, axis=1)
        arrived = [from_behind(piece, "tm", offset) for piece in pieces]
        total = jnp.concatenate(
            [piece + product(power, got) for piece, got in zip(pieces, arrived)], axis=1
        )
        offset *= 2
        if offset < peers:
            power = product(power, power)
    return total[None]


def solution(mesh):
    return jax.shard_map(
        shards,
        mesh=mesh,
        in_specs=(
            P("tm", None, "space"),
            P(),
            P(),
            P(),
            P(None, "space"),
            P(None, "space"),
            P("space"),
            P("space"),
        ),
        out_specs=P("tm", None, "space"),
        check_vma=False,
    )
```

```python
import functools

import numpy as np
import jax
import jax.numpy as jnp
from jax import lax
from jax.experimental import pallas as pl
from jax.experimental.pallas import tpu as pltpu
from jax.sharding import PartitionSpec as P

STEPS = 3
LANES = 128
UNROLL = 8
SCAN_PIECES = 4


time_step = 0.05


def from_behind(shard, axis, by):
    peers = lax.axis_size(axis)
    pairs = [(i, i + by) for i in range(peers) if 0 <= i + by < peers]
    return lax.ppermute(shard, axis, pairs)


def ring(shard, axis, by):
    peers = lax.axis_size(axis)
    return lax.ppermute(shard, axis, [(i, (i + by) % peers) for i in range(peers)])


def product(matrix, vector):
    return jnp.dot(
        matrix, vector, precision=lax.Precision.HIGHEST, preferred_element_type=jnp.float32
    )


def face_nodes():
    i, j, k = np.meshgrid(np.arange(4), np.arange(4), np.arange(4), indexing="ij")
    node = 16 * i + 4 * j + k
    return [
        node[0].ravel(), node[3].ravel(),
        node[:, 0].ravel(), node[:, 3].ravel(),
        node[:, :, 0].ravel(), node[:, :, 3].ravel(),
    ]


def orientations():
    base = np.arange(16).reshape(4, 4)
    out = []
    for code in range(8):
        turned = base
        if code & 4:
            turned = turned.T
        if code & 1:
            turned = turned[::-1]
        if code & 2:
            turned = turned[:, ::-1]
        out.append(turned.ravel())
    return out


def selection_tables():
    nodes, perms = face_nodes(), orientations()
    pick = np.zeros((6, LANES, LANES), np.float32)
    own = np.zeros((64, 96), np.float32)
    for f in range(6):
        for code in range(8):
            for q in range(16):
                pick[f, nodes[f ^ 1][perms[code][q]], 16 * code + q] = 1.0
        for m in range(16):
            own[nodes[f][m], 16 * f + m] = 1.0
    return pick, own


def gather_kernel(idx_ref, table_ref, out_ref):
    def body(step, carry):
        for u in range(UNROLL):
            row = step * UNROLL + u
            out_ref[pl.ds(row, 1), :] = table_ref[pl.ds(idx_ref[row], 1), :]
        return carry

    lax.fori_loop(0, out_ref.shape[0] // UNROLL, body, 0)


def gather_rows(table, idx):
    moved = 4 * table.shape[1] * (2 * idx.shape[0] + table.shape[0])
    return pl.pallas_call(
        gather_kernel,
        out_shape=jax.ShapeDtypeStruct((idx.shape[0], table.shape[1]), table.dtype),
        cost_estimate=pl.CostEstimate(flops=0, transcendentals=0, bytes_accessed=moved),
        in_specs=[
            pl.BlockSpec(memory_space=pltpu.SMEM),
            pl.BlockSpec(memory_space=pltpu.VMEM),
        ],
        out_specs=pl.BlockSpec(memory_space=pltpu.VMEM),
    )(idx, table)


def fine_step(state, folded, pick, spread, mask, near_rows, far_rows, send_rows):
    elements = state.shape[0]
    padded = jnp.pad(state, ((0, 0), (0, LANES - state.shape[1])))
    sent = gather_rows(padded, send_rows)
    half = sent.shape[0] // 2
    low_trace = sent[:half, 0:16].T
    high_trace = sent[half:, 48:64].T
    before = ring(high_trace, "space", 1)
    after = ring(low_trace, "space", -1)
    beside_near = gather_rows(padded, near_rows).reshape(4, elements, LANES)
    halo_low = jnp.pad(before.T, ((0, 0), (48, LANES - 64)))
    halo_high = jnp.pad(after.T, ((0, 0), (0, LANES - 16)))
    table = jnp.concatenate([padded, halo_low, halo_high], axis=0)
    beside_far = gather_rows(table, far_rows).reshape(2, elements, LANES)
    lifted = 0.0
    for beside, faces in ((beside_far, slice(0, 2)), (beside_near, slice(2, 6))):
        turned = jnp.einsum(
            "fer,frq->feq", beside, pick[faces], precision=lax.Precision.HIGHEST,
            preferred_element_type=jnp.float32,
        )
        chosen = jnp.where(mask[faces], turned, 0.0)
        lifted = lifted + jnp.einsum(
            "feq,fqn->en", chosen, spread[faces], precision=lax.Precision.HIGHEST,
            preferred_element_type=jnp.float32,
        )
    rate = product(state, folded) + lifted + state - state * state * state
    return state + time_step * rate


def shards(start_state, stiffness, lifting, coarse, neighbor, orientation, send_low, send_high):
    pick_np, own_np = selection_tables()
    pick = jnp.asarray(pick_np)
    own = jnp.asarray(own_np)
    lift_t = lifting.T.reshape(6, 16, 64)
    spread = jnp.broadcast_to(lift_t[:, None], (6, 8, 16, 64)).reshape(6, LANES, 64)
    folded = stiffness.T - product(own, lifting.T)
    lane_code = jnp.arange(LANES, dtype=jnp.int32) // 16
    mask = orientation[:, :, None] == lane_code[None, None, :]
    far_rows = neighbor[:2].reshape(-1)
    near_rows = neighbor[2:].reshape(-1)
    send_rows = jnp.concatenate([send_low, send_high])

    state_start = start_state[0]
    fine_state = state_start.T
    for step_id in range(STEPS):
        fine_state = fine_step(
            fine_state, folded, pick, spread, mask, near_rows, far_rows, send_rows
        )
    fine_state = fine_state.T
    coarse_start = product(coarse, state_start)
    defect = fine_state - coarse_start
    is_first = lax.axis_index("tm") == 0
    total = jnp.where(is_first, coarse_start + defect, defect)
    power = coarse
    offset = 1
    peers = lax.axis_size("tm")
    while offset < peers:
        pieces = jnp.split(total, SCAN_PIECES, axis=1)
        arrived = [from_behind(piece, "tm", offset) for piece in pieces]
        total = jnp.concatenate(
            [piece + product(power, got) for piece, got in zip(pieces, arrived)], axis=1
        )
        offset *= 2
        if offset < peers:
            power = product(power, power)
    return total[None]


def solution(mesh):
    return jax.shard_map(
        shards,
        mesh=mesh,
        in_specs=(
            P("tm", None, "space"),
            P(),
            P(),
            P(),
            P(None, "space"),
            P(None, "space"),
            P("space"),
            P("space"),
        ),
        out_specs=P("tm", None, "space"),
        check_vma=False,
    )
```

```python
import functools

import numpy as np
import jax
import jax.numpy as jnp
from jax import lax
from jax.experimental import pallas as pl
from jax.experimental.pallas import tpu as pltpu
from jax.sharding import PartitionSpec as P

STEPS = 3
LANES = 128
UNROLL = 8
SCAN_PIECES = 4


time_step = 0.05


def from_behind(shard, axis, by):
    peers = lax.axis_size(axis)
    pairs = [(i, i + by) for i in range(peers) if 0 <= i + by < peers]
    return lax.ppermute(shard, axis, pairs)


def ring(shard, axis, by):
    peers = lax.axis_size(axis)
    return lax.ppermute(shard, axis, [(i, (i + by) % peers) for i in range(peers)])


def product(matrix, vector):
    return jnp.dot(
        matrix, vector, precision=lax.Precision.HIGHEST, preferred_element_type=jnp.float32
    )


def face_nodes():
    i, j, k = np.meshgrid(np.arange(4), np.arange(4), np.arange(4), indexing="ij")
    node = 16 * i + 4 * j + k
    return [
        node[0].ravel(), node[3].ravel(),
        node[:, 0].ravel(), node[:, 3].ravel(),
        node[:, :, 0].ravel(), node[:, :, 3].ravel(),
    ]


def orientations():
    base = np.arange(16).reshape(4, 4)
    out = []
    for code in range(8):
        turned = base
        if code & 4:
            turned = turned.T
        if code & 1:
            turned = turned[::-1]
        if code & 2:
            turned = turned[:, ::-1]
        out.append(turned.ravel())
    return out


def selection_tables():
    nodes, perms = face_nodes(), orientations()
    pick = np.zeros((6, LANES, LANES), np.float32)
    own = np.zeros((64, 96), np.float32)
    for f in range(6):
        for code in range(8):
            for q in range(16):
                pick[f, nodes[f ^ 1][perms[code][q]], 16 * code + q] = 1.0
        for m in range(16):
            own[nodes[f][m], 16 * f + m] = 1.0
    return pick, own


def gather_kernel(idx_ref, table_ref, out_ref):
    def body(step, carry):
        for u in range(UNROLL):
            row = step * UNROLL + u
            out_ref[pl.ds(row, 1), :] = table_ref[pl.ds(idx_ref[row], 1), :]
        return carry

    lax.fori_loop(0, out_ref.shape[0] // UNROLL, body, 0)


def gather_rows(table, idx):
    return pl.pallas_call(
        gather_kernel,
        out_shape=jax.ShapeDtypeStruct((idx.shape[0], table.shape[1]), table.dtype),
        in_specs=[
            pl.BlockSpec(memory_space=pltpu.SMEM),
            pl.BlockSpec(memory_space=pltpu.VMEM),
        ],
        out_specs=pl.BlockSpec(memory_space=pltpu.VMEM),
    )(idx, table)


def fused_kernel(with_send, idx_ref, send_ref, state_ref, halo_ref, mask_ref, pick_ref,
                 spread_ref, folded_ref, out_ref, *rest):
    if with_send:
        sent_ref, table, beside = rest
    else:
        table, beside = rest
    elements = state_ref.shape[0]
    table[0:elements, :] = state_ref[...]
    table[elements:, :] = halo_ref[...]

    def gather(step, carry):
        for u in range(UNROLL):
            row = step * UNROLL + u
            beside[pl.ds(row, 1), :] = table[pl.ds(idx_ref[row], 1), :]
        return carry

    lax.fori_loop(0, beside.shape[0] // UNROLL, gather, 0)
    state = state_ref[...]
    lifted = jnp.zeros_like(state)
    for face in range(6):
        turned = jnp.dot(
            beside[face * elements:(face + 1) * elements, :], pick_ref[face],
            precision=lax.Precision.HIGHEST, preferred_element_type=jnp.float32,
        )
        chosen = jnp.where(mask_ref[face] > 0.5, turned, 0.0)
        lifted = lifted + jnp.dot(
            chosen, spread_ref[face],
            precision=lax.Precision.HIGHEST, preferred_element_type=jnp.float32,
        )
    own = jnp.dot(
        state, folded_ref[...], precision=lax.Precision.HIGHEST,
        preferred_element_type=jnp.float32,
    )
    rate = own + lifted + state - state * state * state
    out_ref[...] = state + time_step * rate
    if with_send:
        def send(step, carry):
            for u in range(UNROLL):
                row = step * UNROLL + u
                sent_ref[pl.ds(row, 1), :] = out_ref[pl.ds(send_ref[row], 1), :]
            return carry

        lax.fori_loop(0, sent_ref.shape[0] // UNROLL, send, 0)


def fused_step(state, halo, mask, pick, spread, folded, nbr_rows, send_rows, with_send):
    elements, lanes = state.shape
    block = jax.ShapeDtypeStruct((elements, lanes), state.dtype)
    shapes = [block]
    if with_send:
        shapes.append(jax.ShapeDtypeStruct((send_rows.shape[0], lanes), state.dtype))
    vmem = pl.BlockSpec(memory_space=pltpu.VMEM)
    smem = pl.BlockSpec(memory_space=pltpu.SMEM)
    flops = 2 * 6 * 6 * elements * lanes * (2 * lanes) + 2 * 6 * elements * lanes * lanes
    moved = 4 * (4 * elements * lanes + mask.size + pick.size + spread.size)
    result = pl.pallas_call(
        functools.partial(fused_kernel, with_send),
        out_shape=tuple(shapes),
        in_specs=[smem, smem] + [vmem] * 6,
        out_specs=tuple([vmem] * len(shapes)),
        scratch_shapes=[
            pltpu.VMEM((elements + halo.shape[0], lanes), jnp.float32),
            pltpu.VMEM((nbr_rows.shape[0], lanes), jnp.float32),
        ],
        cost_estimate=pl.CostEstimate(flops=flops, transcendentals=0, bytes_accessed=moved),
    )(nbr_rows, send_rows, state, halo, mask, pick, spread, folded)
    return result


def shards(start_state, stiffness, lifting, coarse, neighbor, orientation, send_low, send_high):
    pick_np, own_np = selection_tables()
    pick = jnp.asarray(pick_np)
    own = jnp.asarray(own_np)
    lift_t = lifting.T.reshape(6, 16, 64)
    spread = jnp.broadcast_to(lift_t[:, None], (6, 8, 16, 64)).reshape(6, LANES, 64)
    folded = stiffness.T - product(own, lifting.T)
    lane_code = jnp.arange(LANES, dtype=jnp.int32) // 16
    mask = orientation[:, :, None] == lane_code[None, None, :]
    nbr_rows = neighbor.reshape(-1)
    send_rows = jnp.concatenate([send_low, send_high])
    spread = jnp.pad(spread, ((0, 0), (0, 0), (0, LANES - 64)))
    folded = jnp.pad(folded, ((0, LANES - 64), (0, LANES - 64)))
    mask = mask.astype(jnp.float32)

    state_start = start_state[0]
    state = jnp.pad(state_start.T, ((0, 0), (0, LANES - state_start.shape[0])))
    sent = gather_rows(state, send_rows)
    half = send_low.shape[0]
    for step_id in range(STEPS):
        before = ring(sent[half:, 48:64].T, "space", 1)
        after = ring(sent[:half, 0:16].T, "space", -1)
        halo = jnp.concatenate(
            [
                jnp.pad(before.T, ((0, 0), (48, LANES - 64))),
                jnp.pad(after.T, ((0, 0), (0, LANES - 16))),
            ],
            axis=0,
        )
        with_send = step_id < STEPS - 1
        result = fused_step(
            state, halo, mask, pick, spread, folded, nbr_rows, send_rows, with_send
        )
        state = result[0]
        if with_send:
            sent = result[1]
    fine_state = state[:, : state_start.shape[0]].T
    coarse_start = product(coarse, state_start)
    defect = fine_state - coarse_start
    is_first = lax.axis_index("tm") == 0
    total = jnp.where(is_first, coarse_start + defect, defect)
    power = coarse
    offset = 1
    peers = lax.axis_size("tm")
    while offset < peers:
        pieces = jnp.split(total, SCAN_PIECES, axis=1)
        arrived = [from_behind(piece, "tm", offset) for piece in pieces]
        total = jnp.concatenate(
            [piece + product(power, got) for piece, got in zip(pieces, arrived)], axis=1
        )
        offset *= 2
        if offset < peers:
            power = product(power, power)
    return total[None]


def solution(mesh):
    return jax.shard_map(
        shards,
        mesh=mesh,
        in_specs=(
            P("tm", None, "space"),
            P(),
            P(),
            P(),
            P(None, "space"),
            P(None, "space"),
            P("space"),
            P("space"),
        ),
        out_specs=P("tm", None, "space"),
        check_vma=False,
    )
```

```python
import functools

import numpy as np
import jax
import jax.numpy as jnp
from jax import lax
from jax.experimental import pallas as pl
from jax.experimental.pallas import tpu as pltpu
from jax.sharding import PartitionSpec as P

STEPS = 3
LANES = 128
UNROLL = 8


time_step = 0.05


def from_behind(shard, axis, by):
    peers = lax.axis_size(axis)
    pairs = [(i, i + by) for i in range(peers) if 0 <= i + by < peers]
    return lax.ppermute(shard, axis, pairs)


def ring(shard, axis, by):
    peers = lax.axis_size(axis)
    return lax.ppermute(shard, axis, [(i, (i + by) % peers) for i in range(peers)])


def product(matrix, vector):
    return jnp.dot(
        matrix, vector, precision=lax.Precision.HIGHEST, preferred_element_type=jnp.float32
    )


def face_nodes():
    i, j, k = np.meshgrid(np.arange(4), np.arange(4), np.arange(4), indexing="ij")
    node = 16 * i + 4 * j + k
    return [
        node[0].ravel(), node[3].ravel(),
        node[:, 0].ravel(), node[:, 3].ravel(),
        node[:, :, 0].ravel(), node[:, :, 3].ravel(),
    ]


def orientations():
    base = np.arange(16).reshape(4, 4)
    out = []
    for code in range(8):
        turned = base
        if code & 4:
            turned = turned.T
        if code & 1:
            turned = turned[::-1]
        if code & 2:
            turned = turned[:, ::-1]
        out.append(turned.ravel())
    return out


def selection_tables():
    nodes, perms = face_nodes(), orientations()
    pick = np.zeros((6, LANES, LANES), np.float32)
    own = np.zeros((64, 96), np.float32)
    for f in range(6):
        for code in range(8):
            for q in range(16):
                pick[f, nodes[f ^ 1][perms[code][q]], 16 * code + q] = 1.0
        for m in range(16):
            own[nodes[f][m], 16 * f + m] = 1.0
    return pick, own


def gather_kernel(idx_ref, table_ref, out_ref):
    def body(step, carry):
        for u in range(UNROLL):
            row = step * UNROLL + u
            out_ref[pl.ds(row, 1), :] = table_ref[pl.ds(idx_ref[row], 1), :]
        return carry

    lax.fori_loop(0, out_ref.shape[0] // UNROLL, body, 0)


def gather_rows(table, idx):
    return pl.pallas_call(
        gather_kernel,
        out_shape=jax.ShapeDtypeStruct((idx.shape[0], table.shape[1]), table.dtype),
        in_specs=[
            pl.BlockSpec(memory_space=pltpu.SMEM),
            pl.BlockSpec(memory_space=pltpu.VMEM),
        ],
        out_specs=pl.BlockSpec(memory_space=pltpu.VMEM),
    )(idx, table)


def fused_kernel(with_send, idx_ref, send_ref, state_ref, halo_ref, mask_ref, pick_ref,
                 spread_ref, folded_ref, out_ref, *rest):
    if with_send:
        sent_ref, table, beside = rest
    else:
        table, beside = rest
    elements = state_ref.shape[0]
    table[0:elements, :] = state_ref[...]
    table[elements:, :] = halo_ref[...]

    def gather(step, carry):
        for u in range(UNROLL):
            row = step * UNROLL + u
            beside[pl.ds(row, 1), :] = table[pl.ds(idx_ref[row], 1), :]
        return carry

    lax.fori_loop(0, beside.shape[0] // UNROLL, gather, 0)
    state = state_ref[...]
    lifted = jnp.zeros_like(state)
    for face in range(6):
        turned = jnp.dot(
            beside[face * elements:(face + 1) * elements, :], pick_ref[face],
            precision=lax.Precision.HIGHEST, preferred_element_type=jnp.float32,
        )
        chosen = jnp.where(mask_ref[face] > 0.5, turned, 0.0)
        lifted = lifted + jnp.dot(
            chosen, spread_ref[face],
            precision=lax.Precision.HIGHEST, preferred_element_type=jnp.float32,
        )
    own = jnp.dot(
        state, folded_ref[...], precision=lax.Precision.HIGHEST,
        preferred_element_type=jnp.float32,
    )
    rate = own + lifted + state - state * state * state
    out_ref[...] = state + time_step * rate
    if with_send:
        def send(step, carry):
            for u in range(UNROLL):
                row = step * UNROLL + u
                sent_ref[pl.ds(row, 1), :] = out_ref[pl.ds(send_ref[row], 1), :]
            return carry

        lax.fori_loop(0, sent_ref.shape[0] // UNROLL, send, 0)


def fused_step(state, halo, mask, pick, spread, folded, nbr_rows, send_rows, with_send):
    elements, lanes = state.shape
    block = jax.ShapeDtypeStruct((elements, lanes), state.dtype)
    shapes = [block]
    if with_send:
        shapes.append(jax.ShapeDtypeStruct((send_rows.shape[0], lanes), state.dtype))
    vmem = pl.BlockSpec(memory_space=pltpu.VMEM)
    smem = pl.BlockSpec(memory_space=pltpu.SMEM)
    flops = 2 * 6 * 6 * elements * lanes * (2 * lanes) + 2 * 6 * elements * lanes * lanes
    moved = 4 * (4 * elements * lanes + mask.size + pick.size + spread.size)
    result = pl.pallas_call(
        functools.partial(fused_kernel, with_send),
        out_shape=tuple(shapes),
        in_specs=[smem, smem] + [vmem] * 6,
        out_specs=tuple([vmem] * len(shapes)),
        scratch_shapes=[
            pltpu.VMEM((elements + halo.shape[0], lanes), jnp.float32),
            pltpu.VMEM((nbr_rows.shape[0], lanes), jnp.float32),
        ],
        cost_estimate=pl.CostEstimate(flops=flops, transcendentals=0, bytes_accessed=moved),
    )(nbr_rows, send_rows, state, halo, mask, pick, spread, folded)
    return result


def shards(start_state, stiffness, lifting, coarse, neighbor, orientation, send_low, send_high):
    pick_np, own_np = selection_tables()
    pick = jnp.asarray(pick_np)
    own = jnp.asarray(own_np)
    lift_t = lifting.T.reshape(6, 16, 64)
    spread = jnp.broadcast_to(lift_t[:, None], (6, 8, 16, 64)).reshape(6, LANES, 64)
    folded = stiffness.T - product(own, lifting.T)
    lane_code = jnp.arange(LANES, dtype=jnp.int32) // 16
    mask = orientation[:, :, None] == lane_code[None, None, :]
    nbr_rows = neighbor.reshape(-1)
    send_rows = jnp.concatenate([send_low, send_high])
    spread = jnp.pad(spread, ((0, 0), (0, 0), (0, LANES - 64)))
    folded = jnp.pad(folded, ((0, LANES - 64), (0, LANES - 64)))
    mask = mask.astype(jnp.float32)

    state_start = start_state[0]
    state = jnp.pad(state_start.T, ((0, 0), (0, LANES - state_start.shape[0])))
    sent = gather_rows(state, send_rows)
    half = send_low.shape[0]
    for step_id in range(STEPS):
        before = ring(sent[half:, 48:64].T, "space", 1)
        after = ring(sent[:half, 0:16].T, "space", -1)
        halo = jnp.concatenate(
            [
                jnp.pad(before.T, ((0, 0), (48, LANES - 64))),
                jnp.pad(after.T, ((0, 0), (0, LANES - 16))),
            ],
            axis=0,
        )
        with_send = step_id < STEPS - 1
        result = fused_step(
            state, halo, mask, pick, spread, folded, nbr_rows, send_rows, with_send
        )
        state = result[0]
        if with_send:
            sent = result[1]
    fine_state = state[:, : state_start.shape[0]].T
    coarse_start = product(coarse, state_start)
    defect = fine_state - coarse_start
    is_first = lax.axis_index("tm") == 0
    total = jnp.where(is_first, coarse_start + defect, defect)
    return scan_over_time(total, coarse)[None]


def scan_over_time(total, coarse):
    peers = lax.axis_size("tm")
    core = lax.axis_index("tm") % 2
    partner = [(i, i ^ 1) for i in range(peers)]
    half = total.shape[1] // 2
    low, high = total[:, :half], total[:, half:]
    got = lax.ppermute(jnp.where(core == 0, high, low), "tm", partner)
    keep = jnp.where(core == 0, low, high)
    first = jnp.where(core == 0, keep, got)
    second = jnp.where(core == 0, got, keep)
    aggregate = product(coarse, first) + second
    square = product(coarse, coarse)
    before = from_behind(aggregate, "tm", 2)
    power = square
    shift = 1
    while shift < peers // 2:
        before = before + product(power, from_behind(before, "tm", 2 * shift))
        shift *= 2
        if shift < peers // 2:
            power = product(power, power)
    end_first = product(coarse, before) + first
    end_second = product(square, before) + aggregate
    mine = jnp.where(core == 0, end_first, end_second)
    got = lax.ppermute(jnp.where(core == 0, end_second, end_first), "tm", partner)
    return jnp.where(
        core == 0,
        jnp.concatenate([mine, got], axis=1),
        jnp.concatenate([got, mine], axis=1),
    )


def solution(mesh):
    return jax.shard_map(
        shards,
        mesh=mesh,
        in_specs=(
            P("tm", None, "space"),
            P(),
            P(),
            P(),
            P(None, "space"),
            P(None, "space"),
            P("space"),
            P("space"),
        ),
        out_specs=P("tm", None, "space"),
        check_vma=False,
    )
```

```python
import functools

import numpy as np
import jax
import jax.numpy as jnp
from jax import lax
from jax.experimental import pallas as pl
from jax.experimental.pallas import tpu as pltpu
from jax.sharding import PartitionSpec as P

STEPS = 3
LANES = 128
UNROLL = 8


time_step = 0.05


def from_behind(shard, axis, by):
    peers = lax.axis_size(axis)
    pairs = [(i, i + by) for i in range(peers) if 0 <= i + by < peers]
    return lax.ppermute(shard, axis, pairs)


def ring(shard, axis, by):
    peers = lax.axis_size(axis)
    return lax.ppermute(shard, axis, [(i, (i + by) % peers) for i in range(peers)])


def product(matrix, vector):
    return jnp.dot(
        matrix, vector, precision=lax.Precision.HIGHEST, preferred_element_type=jnp.float32
    )


def face_nodes():
    i, j, k = np.meshgrid(np.arange(4), np.arange(4), np.arange(4), indexing="ij")
    node = 16 * i + 4 * j + k
    return [
        node[0].ravel(), node[3].ravel(),
        node[:, 0].ravel(), node[:, 3].ravel(),
        node[:, :, 0].ravel(), node[:, :, 3].ravel(),
    ]


def orientations():
    base = np.arange(16).reshape(4, 4)
    out = []
    for code in range(8):
        turned = base
        if code & 4:
            turned = turned.T
        if code & 1:
            turned = turned[::-1]
        if code & 2:
            turned = turned[:, ::-1]
        out.append(turned.ravel())
    return out


def selection_tables():
    nodes, perms = face_nodes(), orientations()
    pick = np.zeros((6, LANES, LANES), np.float32)
    own = np.zeros((64, 96), np.float32)
    for f in range(6):
        for code in range(8):
            for q in range(16):
                pick[f, nodes[f ^ 1][perms[code][q]], 16 * code + q] = 1.0
        for m in range(16):
            own[nodes[f][m], 16 * f + m] = 1.0
    return pick, own


def gather_kernel(idx_ref, table_ref, out_ref):
    def body(step, carry):
        for u in range(UNROLL):
            row = step * UNROLL + u
            out_ref[pl.ds(row, 1), :] = table_ref[pl.ds(idx_ref[row], 1), :]
        return carry

    lax.fori_loop(0, out_ref.shape[0] // UNROLL, body, 0)


def gather_rows(table, idx):
    return pl.pallas_call(
        gather_kernel,
        out_shape=jax.ShapeDtypeStruct((idx.shape[0], table.shape[1]), table.dtype),
        in_specs=[
            pl.BlockSpec(memory_space=pltpu.SMEM),
            pl.BlockSpec(memory_space=pltpu.VMEM),
        ],
        out_specs=pl.BlockSpec(memory_space=pltpu.VMEM),
    )(idx, table)


def split_three(x):
    high = x.astype(jnp.bfloat16)
    rest = x - high.astype(jnp.float32)
    middle = rest.astype(jnp.bfloat16)
    low = (rest - middle.astype(jnp.float32)).astype(jnp.bfloat16)
    return high, middle, low


def bf16_dot(a, b):
    return jnp.dot(a, b, preferred_element_type=jnp.float32)


def three_pass_dot(a, b):
    a_parts, b_parts = split_three(a), split_three(b)
    return bf16_dot(a_parts[0], b_parts[0]) + (
        bf16_dot(a_parts[0], b_parts[1]) + bf16_dot(a_parts[1], b_parts[0])
    )


def fused_kernel(with_send, idx_ref, send_ref, state_ref, halo_ref, mask_ref, pick_ref,
                 spread_ref, folded_ref, out_ref, *rest):
    if with_send:
        sent_ref, table, beside = rest
    else:
        table, beside = rest
    elements = state_ref.shape[0]
    table[0:elements, :] = state_ref[...]
    table[elements:, :] = halo_ref[...]

    def gather(step, carry):
        for u in range(UNROLL):
            row = step * UNROLL + u
            beside[pl.ds(row, 1), :] = table[pl.ds(idx_ref[row], 1), :]
        return carry

    lax.fori_loop(0, beside.shape[0] // UNROLL, gather, 0)
    state = state_ref[...]
    lifted = jnp.zeros_like(state)
    for face in range(6):
        parts = split_three(beside[face * elements:(face + 1) * elements, :])
        turned = (bf16_dot(parts[0], pick_ref[face]) + bf16_dot(parts[1], pick_ref[face])) + (
            bf16_dot(parts[2], pick_ref[face])
        )
        chosen = jnp.where(mask_ref[face] > 0.5, turned, 0.0)
        lifted = lifted + three_pass_dot(chosen, spread_ref[face])
    own = jnp.dot(
        state, folded_ref[...], precision=lax.Precision.HIGHEST,
        preferred_element_type=jnp.float32,
    )
    rate = own + lifted + state - state * state * state
    out_ref[...] = state + time_step * rate
    if with_send:
        def send(step, carry):
            for u in range(UNROLL):
                row = step * UNROLL + u
                sent_ref[pl.ds(row, 1), :] = out_ref[pl.ds(send_ref[row], 1), :]
            return carry

        lax.fori_loop(0, sent_ref.shape[0] // UNROLL, send, 0)


def fused_step(state, halo, mask, pick, spread, folded, nbr_rows, send_rows, with_send):
    elements, lanes = state.shape
    block = jax.ShapeDtypeStruct((elements, lanes), state.dtype)
    shapes = [block]
    if with_send:
        shapes.append(jax.ShapeDtypeStruct((send_rows.shape[0], lanes), state.dtype))
    vmem = pl.BlockSpec(memory_space=pltpu.VMEM)
    smem = pl.BlockSpec(memory_space=pltpu.SMEM)
    flops = 2 * 6 * 6 * elements * lanes * (2 * lanes) + 2 * 6 * elements * lanes * lanes
    moved = 4 * (4 * elements * lanes + mask.size + pick.size + spread.size)
    result = pl.pallas_call(
        functools.partial(fused_kernel, with_send),
        out_shape=tuple(shapes),
        in_specs=[smem, smem] + [vmem] * 6,
        out_specs=tuple([vmem] * len(shapes)),
        scratch_shapes=[
            pltpu.VMEM((elements + halo.shape[0], lanes), jnp.float32),
            pltpu.VMEM((nbr_rows.shape[0], lanes), jnp.float32),
        ],
        cost_estimate=pl.CostEstimate(flops=flops, transcendentals=0, bytes_accessed=moved),
    )(nbr_rows, send_rows, state, halo, mask, pick, spread, folded)
    return result


def shards(start_state, stiffness, lifting, coarse, neighbor, orientation, send_low, send_high):
    pick_np, own_np = selection_tables()
    pick = jnp.asarray(pick_np, dtype=jnp.bfloat16)
    own = jnp.asarray(own_np)
    lift_t = lifting.T.reshape(6, 16, 64)
    spread = jnp.broadcast_to(lift_t[:, None], (6, 8, 16, 64)).reshape(6, LANES, 64)
    folded = stiffness.T - product(own, lifting.T)
    lane_code = jnp.arange(LANES, dtype=jnp.int32) // 16
    mask = orientation[:, :, None] == lane_code[None, None, :]
    nbr_rows = neighbor.reshape(-1)
    send_rows = jnp.concatenate([send_low, send_high])
    spread = jnp.pad(spread, ((0, 0), (0, 0), (0, LANES - 64)))
    folded = jnp.pad(folded, ((0, LANES - 64), (0, LANES - 64)))
    mask = mask.astype(jnp.float32)

    state_start = start_state[0]
    state = jnp.pad(state_start.T, ((0, 0), (0, LANES - state_start.shape[0])))
    sent = gather_rows(state, send_rows)
    half = send_low.shape[0]
    for step_id in range(STEPS):
        before = ring(sent[half:, 48:64].T, "space", 1)
        after = ring(sent[:half, 0:16].T, "space", -1)
        halo = jnp.concatenate(
            [
                jnp.pad(before.T, ((0, 0), (48, LANES - 64))),
                jnp.pad(after.T, ((0, 0), (0, LANES - 16))),
            ],
            axis=0,
        )
        with_send = step_id < STEPS - 1
        result = fused_step(
            state, halo, mask, pick, spread, folded, nbr_rows, send_rows, with_send
        )
        state = result[0]
        if with_send:
            sent = result[1]
    fine_state = state[:, : state_start.shape[0]].T
    coarse_start = product(coarse, state_start)
    defect = fine_state - coarse_start
    is_first = lax.axis_index("tm") == 0
    total = jnp.where(is_first, coarse_start + defect, defect)
    return scan_over_time(total, coarse)[None]


def scan_over_time(total, coarse):
    peers = lax.axis_size("tm")
    core = lax.axis_index("tm") % 2
    partner = [(i, i ^ 1) for i in range(peers)]
    half = total.shape[1] // 2
    low, high = total[:, :half], total[:, half:]
    got = lax.ppermute(jnp.where(core == 0, high, low), "tm", partner)
    keep = jnp.where(core == 0, low, high)
    first = jnp.where(core == 0, keep, got)
    second = jnp.where(core == 0, got, keep)
    aggregate = product(coarse, first) + second
    square = product(coarse, coarse)
    before = from_behind(aggregate, "tm", 2)
    power = square
    shift = 1
    while shift < peers // 2:
        before = before + product(power, from_behind(before, "tm", 2 * shift))
        shift *= 2
        if shift < peers // 2:
            power = product(power, power)
    end_first = product(coarse, before) + first
    end_second = product(square, before) + aggregate
    mine = jnp.where(core == 0, end_first, end_second)
    got = lax.ppermute(jnp.where(core == 0, end_second, end_first), "tm", partner)
    return jnp.where(
        core == 0,
        jnp.concatenate([mine, got], axis=1),
        jnp.concatenate([got, mine], axis=1),
    )


def solution(mesh):
    return jax.shard_map(
        shards,
        mesh=mesh,
        in_specs=(
            P("tm", None, "space"),
            P(),
            P(),
            P(),
            P(None, "space"),
            P(None, "space"),
            P("space"),
            P("space"),
        ),
        out_specs=P("tm", None, "space"),
        check_vma=False,
    )
```

```python
import functools

import numpy as np
import jax
import jax.numpy as jnp
from jax import lax
from jax.experimental import pallas as pl
from jax.experimental.pallas import tpu as pltpu
from jax.sharding import PartitionSpec as P

STEPS = 3
LANES = 128
UNROLL = 8


time_step = 0.05


def from_behind(shard, axis, by):
    peers = lax.axis_size(axis)
    pairs = [(i, i + by) for i in range(peers) if 0 <= i + by < peers]
    return lax.ppermute(shard, axis, pairs)


def ring(shard, axis, by):
    peers = lax.axis_size(axis)
    return lax.ppermute(shard, axis, [(i, (i + by) % peers) for i in range(peers)])


def product(matrix, vector):
    return jnp.dot(
        matrix, vector, precision=lax.Precision.HIGHEST, preferred_element_type=jnp.float32
    )


def face_nodes():
    i, j, k = np.meshgrid(np.arange(4), np.arange(4), np.arange(4), indexing="ij")
    node = 16 * i + 4 * j + k
    return [
        node[0].ravel(), node[3].ravel(),
        node[:, 0].ravel(), node[:, 3].ravel(),
        node[:, :, 0].ravel(), node[:, :, 3].ravel(),
    ]


def orientations():
    base = np.arange(16).reshape(4, 4)
    out = []
    for code in range(8):
        turned = base
        if code & 4:
            turned = turned.T
        if code & 1:
            turned = turned[::-1]
        if code & 2:
            turned = turned[:, ::-1]
        out.append(turned.ravel())
    return out


def selection_tables():
    nodes, perms = face_nodes(), orientations()
    pick = np.zeros((6, LANES, LANES), np.float32)
    own = np.zeros((64, 96), np.float32)
    for f in range(6):
        for code in range(8):
            for q in range(16):
                pick[f, nodes[f ^ 1][perms[code][q]], 16 * code + q] = 1.0
        for m in range(16):
            own[nodes[f][m], 16 * f + m] = 1.0
    return pick, own


def gather_kernel(idx_ref, table_ref, out_ref):
    def body(step, carry):
        for u in range(UNROLL):
            row = step * UNROLL + u
            out_ref[pl.ds(row, 1), :] = table_ref[pl.ds(idx_ref[row], 1), :]
        return carry

    lax.fori_loop(0, out_ref.shape[0] // UNROLL, body, 0)


def gather_rows(table, idx):
    return pl.pallas_call(
        gather_kernel,
        out_shape=jax.ShapeDtypeStruct((idx.shape[0], table.shape[1]), table.dtype),
        in_specs=[
            pl.BlockSpec(memory_space=pltpu.SMEM),
            pl.BlockSpec(memory_space=pltpu.VMEM),
        ],
        out_specs=pl.BlockSpec(memory_space=pltpu.VMEM),
    )(idx, table)


def split_three(x):
    high = x.astype(jnp.bfloat16)
    rest = x - high.astype(jnp.float32)
    middle = rest.astype(jnp.bfloat16)
    low = (rest - middle.astype(jnp.float32)).astype(jnp.bfloat16)
    return high, middle, low


def bf16_dot(a, b):
    return jnp.dot(a, b, preferred_element_type=jnp.float32)


def three_pass_dot(a, b):
    a_parts, b_parts = split_three(a), split_three(b)
    return bf16_dot(a_parts[0], b_parts[0]) + (
        bf16_dot(a_parts[0], b_parts[1]) + bf16_dot(a_parts[1], b_parts[0])
    )


def gather_into(idx_ref, table, beside):
    def gather(step, carry):
        for u in range(UNROLL):
            row = step * UNROLL + u
            beside[pl.ds(row, 1), :] = table[pl.ds(idx_ref[row], 1), :]
        return carry

    lax.fori_loop(0, beside.shape[0] // UNROLL, gather, 0)


def lift_faces(beside, mask_ref, pick_ref, spread_ref, elements, lifted):
    for face in range(pick_ref.shape[0]):
        parts = split_three(beside[face * elements:(face + 1) * elements, :])
        turned = (bf16_dot(parts[0], pick_ref[face]) + bf16_dot(parts[1], pick_ref[face])) + (
            bf16_dot(parts[2], pick_ref[face])
        )
        chosen = jnp.where(mask_ref[face] > 0.5, turned, 0.0)
        lifted = lifted + three_pass_dot(chosen, spread_ref[face])
    return lifted


def near_kernel(idx_ref, state_ref, mask_ref, pick_ref, spread_ref, folded_ref, out_ref, beside):
    elements = state_ref.shape[0]
    gather_into(idx_ref, state_ref, beside)
    own = jnp.dot(
        state_ref[...], folded_ref[...], precision=lax.Precision.HIGHEST,
        preferred_element_type=jnp.float32,
    )
    out_ref[...] = lift_faces(beside, mask_ref, pick_ref, spread_ref, elements, own)


def far_kernel(with_send, idx_ref, send_ref, state_ref, halo_ref, partial_ref, mask_ref,
               pick_ref, spread_ref, out_ref, *rest):
    if with_send:
        sent_ref, table, beside = rest
    else:
        table, beside = rest
    elements = state_ref.shape[0]
    table[0:elements, :] = state_ref[...]
    table[elements:, :] = halo_ref[...]
    gather_into(idx_ref, table, beside)
    state = state_ref[...]
    lifted = lift_faces(beside, mask_ref, pick_ref, spread_ref, elements, partial_ref[...])
    rate = lifted + state - state * state * state
    out_ref[...] = state + time_step * rate
    if with_send:
        def send(step, carry):
            for u in range(UNROLL):
                row = step * UNROLL + u
                sent_ref[pl.ds(row, 1), :] = out_ref[pl.ds(send_ref[row], 1), :]
            return carry

        lax.fori_loop(0, sent_ref.shape[0] // UNROLL, send, 0)


def near_part(state, mask, pick, spread, folded, rows):
    elements, lanes = state.shape
    vmem = pl.BlockSpec(memory_space=pltpu.VMEM)
    faces = pick.shape[0]
    flops = 2 * 6 * faces * elements * lanes * (2 * lanes) + 2 * 6 * elements * lanes * lanes
    moved = 4 * (2 * elements * lanes + mask.size + pick.size + spread.size)
    return pl.pallas_call(
        near_kernel,
        out_shape=jax.ShapeDtypeStruct((elements, lanes), state.dtype),
        in_specs=[pl.BlockSpec(memory_space=pltpu.SMEM)] + [vmem] * 5,
        out_specs=vmem,
        scratch_shapes=[pltpu.VMEM((rows.shape[0], lanes), jnp.float32)],
        cost_estimate=pl.CostEstimate(flops=flops, transcendentals=0, bytes_accessed=moved),
    )(rows, state, mask, pick, spread, folded)


def far_part(state, halo, partial, mask, pick, spread, rows, send_rows, with_send):
    elements, lanes = state.shape
    block = jax.ShapeDtypeStruct((elements, lanes), state.dtype)
    shapes = [block]
    if with_send:
        shapes.append(jax.ShapeDtypeStruct((send_rows.shape[0], lanes), state.dtype))
    vmem = pl.BlockSpec(memory_space=pltpu.VMEM)
    smem = pl.BlockSpec(memory_space=pltpu.SMEM)
    faces = pick.shape[0]
    flops = 2 * 6 * faces * elements * lanes * (2 * lanes)
    moved = 4 * (5 * elements * lanes + mask.size + pick.size + spread.size)
    return pl.pallas_call(
        functools.partial(far_kernel, with_send),
        out_shape=tuple(shapes),
        in_specs=[smem, smem] + [vmem] * 6,
        out_specs=tuple([vmem] * len(shapes)),
        scratch_shapes=[
            pltpu.VMEM((elements + halo.shape[0], lanes), jnp.float32),
            pltpu.VMEM((rows.shape[0], lanes), jnp.float32),
        ],
        cost_estimate=pl.CostEstimate(flops=flops, transcendentals=0, bytes_accessed=moved),
    )(rows, send_rows, state, halo, partial, mask, pick, spread)


def shards(start_state, stiffness, lifting, coarse, neighbor, orientation, send_low, send_high):
    pick_np, own_np = selection_tables()
    pick = jnp.asarray(pick_np, dtype=jnp.bfloat16)
    own = jnp.asarray(own_np)
    lift_t = lifting.T.reshape(6, 16, 64)
    spread = jnp.broadcast_to(lift_t[:, None], (6, 8, 16, 64)).reshape(6, LANES, 64)
    folded = stiffness.T - product(own, lifting.T)
    lane_code = jnp.arange(LANES, dtype=jnp.int32) // 16
    mask = orientation[:, :, None] == lane_code[None, None, :]
    far_rows = neighbor[:2].reshape(-1)
    near_rows = neighbor[2:].reshape(-1)
    send_rows = jnp.concatenate([send_low, send_high])
    spread = jnp.pad(spread, ((0, 0), (0, 0), (0, LANES - 64)))
    folded = jnp.pad(folded, ((0, LANES - 64), (0, LANES - 64)))
    mask = mask.astype(jnp.float32)

    state_start = start_state[0]
    state = jnp.pad(state_start.T, ((0, 0), (0, LANES - state_start.shape[0])))
    sent = gather_rows(state, send_rows)
    half = send_low.shape[0]
    for step_id in range(STEPS):
        before = ring(sent[half:, 48:64].T, "space", 1)
        after = ring(sent[:half, 0:16].T, "space", -1)
        partial = near_part(state, mask[2:], pick[2:], spread[2:], folded, near_rows)
        halo = jnp.concatenate(
            [
                jnp.pad(before.T, ((0, 0), (48, LANES - 64))),
                jnp.pad(after.T, ((0, 0), (0, LANES - 16))),
            ],
            axis=0,
        )
        with_send = step_id < STEPS - 1
        result = far_part(
            state, halo, partial, mask[:2], pick[:2], spread[:2], far_rows, send_rows, with_send
        )
        state = result[0]
        if with_send:
            sent = result[1]
    fine_state = state[:, : state_start.shape[0]].T
    coarse_start = product(coarse, state_start)
    defect = fine_state - coarse_start
    is_first = lax.axis_index("tm") == 0
    total = jnp.where(is_first, coarse_start + defect, defect)
    return scan_over_time(total, coarse)[None]


def scan_over_time(total, coarse):
    peers = lax.axis_size("tm")
    core = lax.axis_index("tm") % 2
    partner = [(i, i ^ 1) for i in range(peers)]
    half = total.shape[1] // 2
    low, high = total[:, :half], total[:, half:]
    got = lax.ppermute(jnp.where(core == 0, high, low), "tm", partner)
    keep = jnp.where(core == 0, low, high)
    first = jnp.where(core == 0, keep, got)
    second = jnp.where(core == 0, got, keep)
    aggregate = product(coarse, first) + second
    square = product(coarse, coarse)
    before = from_behind(aggregate, "tm", 2)
    power = square
    shift = 1
    while shift < peers // 2:
        before = before + product(power, from_behind(before, "tm", 2 * shift))
        shift *= 2
        if shift < peers // 2:
            power = product(power, power)
    end_first = product(coarse, before) + first
    end_second = product(square, before) + aggregate
    mine = jnp.where(core == 0, end_first, end_second)
    got = lax.ppermute(jnp.where(core == 0, end_second, end_first), "tm", partner)
    return jnp.where(
        core == 0,
        jnp.concatenate([mine, got], axis=1),
        jnp.concatenate([got, mine], axis=1),
    )


def solution(mesh):
    return jax.shard_map(
        shards,
        mesh=mesh,
        in_specs=(
            P("tm", None, "space"),
            P(),
            P(),
            P(),
            P(None, "space"),
            P(None, "space"),
            P("space"),
            P("space"),
        ),
        out_specs=P("tm", None, "space"),
        check_vma=False,
    )
```

```python
import functools

import numpy as np
import jax
import jax.numpy as jnp
from jax import lax
from jax.experimental import pallas as pl
from jax.experimental.pallas import tpu as pltpu
from jax.sharding import PartitionSpec as P

STEPS = 3
LANES = 128
UNROLL = 8


time_step = 0.05


def from_behind(shard, axis, by):
    peers = lax.axis_size(axis)
    pairs = [(i, i + by) for i in range(peers) if 0 <= i + by < peers]
    return lax.ppermute(shard, axis, pairs)


def ring(shard, axis, by):
    peers = lax.axis_size(axis)
    return lax.ppermute(shard, axis, [(i, (i + by) % peers) for i in range(peers)])


def product(matrix, vector):
    return jnp.dot(
        matrix, vector, precision=lax.Precision.HIGHEST, preferred_element_type=jnp.float32
    )


def face_nodes():
    i, j, k = np.meshgrid(np.arange(4), np.arange(4), np.arange(4), indexing="ij")
    node = 16 * i + 4 * j + k
    return [
        node[0].ravel(), node[3].ravel(),
        node[:, 0].ravel(), node[:, 3].ravel(),
        node[:, :, 0].ravel(), node[:, :, 3].ravel(),
    ]


def orientations():
    base = np.arange(16).reshape(4, 4)
    out = []
    for code in range(8):
        turned = base
        if code & 4:
            turned = turned.T
        if code & 1:
            turned = turned[::-1]
        if code & 2:
            turned = turned[:, ::-1]
        out.append(turned.ravel())
    return out


def selection_tables():
    nodes, perms = face_nodes(), orientations()
    pick = np.zeros((6, LANES, LANES), np.float32)
    own = np.zeros((64, 96), np.float32)
    for f in range(6):
        for code in range(8):
            for q in range(16):
                pick[f, nodes[f ^ 1][perms[code][q]], 16 * code + q] = 1.0
        for m in range(16):
            own[nodes[f][m], 16 * f + m] = 1.0
    return pick, own


def gather_kernel(idx_ref, table_ref, out_ref):
    def body(step, carry):
        for u in range(UNROLL):
            row = step * UNROLL + u
            out_ref[pl.ds(row, 1), :] = table_ref[pl.ds(idx_ref[row], 1), :]
        return carry

    lax.fori_loop(0, out_ref.shape[0] // UNROLL, body, 0)


def gather_rows(table, idx):
    return pl.pallas_call(
        gather_kernel,
        out_shape=jax.ShapeDtypeStruct((idx.shape[0], table.shape[1]), table.dtype),
        in_specs=[
            pl.BlockSpec(memory_space=pltpu.SMEM),
            pl.BlockSpec(memory_space=pltpu.VMEM),
        ],
        out_specs=pl.BlockSpec(memory_space=pltpu.VMEM),
    )(idx, table)


def split_three(x):
    high = x.astype(jnp.bfloat16)
    rest = x - high.astype(jnp.float32)
    middle = rest.astype(jnp.bfloat16)
    low = (rest - middle.astype(jnp.float32)).astype(jnp.bfloat16)
    return high, middle, low


def bf16_dot(a, b):
    return jnp.dot(a, b, preferred_element_type=jnp.float32)


def three_pass_dot(a, b):
    a_parts, b_parts = split_three(a), split_three(b)
    return bf16_dot(a_parts[0], b_parts[0]) + (
        bf16_dot(a_parts[0], b_parts[1]) + bf16_dot(a_parts[1], b_parts[0])
    )


def fused_kernel(with_send, idx_ref, send_ref, state_ref, halo_ref, mask_ref, pick_ref,
                 spread_ref, folded_ref, out_ref, *rest):
    if with_send:
        sent_ref, table, beside = rest
    else:
        table, beside = rest
    elements = state_ref.shape[0]
    table[0:elements, :] = state_ref[...]
    table[elements:, :] = halo_ref[...]

    def gather(step, carry):
        for u in range(UNROLL):
            row = step * UNROLL + u
            beside[pl.ds(row, 1), :] = table[pl.ds(idx_ref[row], 1), :]
        return carry

    lax.fori_loop(0, beside.shape[0] // UNROLL, gather, 0)
    state = state_ref[...]
    lifted = jnp.zeros_like(state)
    lane_code = lax.broadcasted_iota(jnp.int32, state.shape, 1) // 16
    for face in range(6):
        parts = split_three(beside[face * elements:(face + 1) * elements, :])
        turned = (bf16_dot(parts[0], pick_ref[face]) + bf16_dot(parts[1], pick_ref[face])) + (
            bf16_dot(parts[2], pick_ref[face])
        )
        chosen = jnp.where(mask_ref[face] == lane_code, turned, 0.0)
        lifted = lifted + three_pass_dot(chosen, spread_ref[face])
    own = jnp.dot(
        state, folded_ref[...], precision=lax.Precision.HIGHEST,
        preferred_element_type=jnp.float32,
    )
    rate = own + lifted + state - state * state * state
    out_ref[...] = state + time_step * rate
    if with_send:
        def send(step, carry):
            for u in range(UNROLL):
                row = step * UNROLL + u
                sent_ref[pl.ds(row, 1), :] = out_ref[pl.ds(send_ref[row], 1), :]
            return carry

        lax.fori_loop(0, sent_ref.shape[0] // UNROLL, send, 0)


def fused_step(state, halo, mask, pick, spread, folded, nbr_rows, send_rows, with_send):
    elements, lanes = state.shape
    block = jax.ShapeDtypeStruct((elements, lanes), state.dtype)
    shapes = [block]
    if with_send:
        shapes.append(jax.ShapeDtypeStruct((send_rows.shape[0], lanes), state.dtype))
    vmem = pl.BlockSpec(memory_space=pltpu.VMEM)
    smem = pl.BlockSpec(memory_space=pltpu.SMEM)
    flops = 2 * 6 * 6 * elements * lanes * (2 * lanes) + 2 * 6 * elements * lanes * lanes
    moved = 4 * (4 * elements * lanes + mask.size + pick.size + spread.size)
    result = pl.pallas_call(
        functools.partial(fused_kernel, with_send),
        out_shape=tuple(shapes),
        in_specs=[smem, smem] + [vmem] * 6,
        out_specs=tuple([vmem] * len(shapes)),
        scratch_shapes=[
            pltpu.VMEM((elements + halo.shape[0], lanes), jnp.float32),
            pltpu.VMEM((nbr_rows.shape[0], lanes), jnp.float32),
        ],
        cost_estimate=pl.CostEstimate(flops=flops, transcendentals=0, bytes_accessed=moved),
    )(nbr_rows, send_rows, state, halo, mask, pick, spread, folded)
    return result


def shards(start_state, stiffness, lifting, coarse, neighbor, orientation, send_low, send_high):
    pick_np, own_np = selection_tables()
    pick = jnp.asarray(pick_np, dtype=jnp.bfloat16)
    own = jnp.asarray(own_np)
    lift_t = lifting.T.reshape(6, 16, 64)
    spread = jnp.broadcast_to(lift_t[:, None], (6, 8, 16, 64)).reshape(6, LANES, 64)
    folded = stiffness.T - product(own, lifting.T)
    mask = orientation[:, :, None]
    nbr_rows = neighbor.reshape(-1)
    send_rows = jnp.concatenate([send_low, send_high])
    spread = jnp.pad(spread, ((0, 0), (0, 0), (0, LANES - 64)))
    folded = jnp.pad(folded, ((0, LANES - 64), (0, LANES - 64)))

    state_start = start_state[0]
    state = jnp.pad(state_start.T, ((0, 0), (0, LANES - state_start.shape[0])))
    sent = gather_rows(state, send_rows)
    half = send_low.shape[0]
    for step_id in range(STEPS):
        before = ring(sent[half:, 48:64].T, "space", 1)
        after = ring(sent[:half, 0:16].T, "space", -1)
        halo = jnp.concatenate(
            [
                jnp.pad(before.T, ((0, 0), (48, LANES - 64))),
                jnp.pad(after.T, ((0, 0), (0, LANES - 16))),
            ],
            axis=0,
        )
        with_send = step_id < STEPS - 1
        result = fused_step(
            state, halo, mask, pick, spread, folded, nbr_rows, send_rows, with_send
        )
        state = result[0]
        if with_send:
            sent = result[1]
    fine_state = state[:, : state_start.shape[0]].T
    coarse_start = product(coarse, state_start)
    defect = fine_state - coarse_start
    is_first = lax.axis_index("tm") == 0
    total = jnp.where(is_first, coarse_start + defect, defect)
    return scan_over_time(total, coarse)[None]


def scan_over_time(total, coarse):
    peers = lax.axis_size("tm")
    core = lax.axis_index("tm") % 2
    partner = [(i, i ^ 1) for i in range(peers)]
    half = total.shape[1] // 2
    low, high = total[:, :half], total[:, half:]
    got = lax.ppermute(jnp.where(core == 0, high, low), "tm", partner)
    keep = jnp.where(core == 0, low, high)
    first = jnp.where(core == 0, keep, got)
    second = jnp.where(core == 0, got, keep)
    aggregate = product(coarse, first) + second
    square = product(coarse, coarse)
    before = from_behind(aggregate, "tm", 2)
    power = square
    shift = 1
    while shift < peers // 2:
        before = before + product(power, from_behind(before, "tm", 2 * shift))
        shift *= 2
        if shift < peers // 2:
            power = product(power, power)
    end_first = product(coarse, before) + first
    end_second = product(square, before) + aggregate
    mine = jnp.where(core == 0, end_first, end_second)
    got = lax.ppermute(jnp.where(core == 0, end_second, end_first), "tm", partner)
    return jnp.where(
        core == 0,
        jnp.concatenate([mine, got], axis=1),
        jnp.concatenate([got, mine], axis=1),
    )


def solution(mesh):
    return jax.shard_map(
        shards,
        mesh=mesh,
        in_specs=(
            P("tm", None, "space"),
            P(),
            P(),
            P(),
            P(None, "space"),
            P(None, "space"),
            P("space"),
            P("space"),
        ),
        out_specs=P("tm", None, "space"),
        check_vma=False,
    )
```

```python
import functools

import numpy as np
import jax
import jax.numpy as jnp
from jax import lax
from jax.experimental import pallas as pl
from jax.experimental.pallas import tpu as pltpu
from jax.sharding import PartitionSpec as P

STEPS = 3
LANES = 128
UNROLL = 64


time_step = 0.05


def from_behind(shard, axis, by):
    peers = lax.axis_size(axis)
    pairs = [(i, i + by) for i in range(peers) if 0 <= i + by < peers]
    return lax.ppermute(shard, axis, pairs)


def ring(shard, axis, by):
    peers = lax.axis_size(axis)
    return lax.ppermute(shard, axis, [(i, (i + by) % peers) for i in range(peers)])


def product(matrix, vector):
    return jnp.dot(
        matrix, vector, precision=lax.Precision.HIGHEST, preferred_element_type=jnp.float32
    )


def face_nodes():
    i, j, k = np.meshgrid(np.arange(4), np.arange(4), np.arange(4), indexing="ij")
    node = 16 * i + 4 * j + k
    return [
        node[0].ravel(), node[3].ravel(),
        node[:, 0].ravel(), node[:, 3].ravel(),
        node[:, :, 0].ravel(), node[:, :, 3].ravel(),
    ]


def orientations():
    base = np.arange(16).reshape(4, 4)
    out = []
    for code in range(8):
        turned = base
        if code & 4:
            turned = turned.T
        if code & 1:
            turned = turned[::-1]
        if code & 2:
            turned = turned[:, ::-1]
        out.append(turned.ravel())
    return out


def selection_tables():
    nodes, perms = face_nodes(), orientations()
    pick = np.zeros((6, LANES, LANES), np.float32)
    own = np.zeros((64, 96), np.float32)
    for f in range(6):
        for code in range(8):
            for q in range(16):
                pick[f, nodes[f ^ 1][perms[code][q]], 16 * code + q] = 1.0
        for m in range(16):
            own[nodes[f][m], 16 * f + m] = 1.0
    return pick, own


def gather_kernel(idx_ref, table_ref, out_ref):
    def body(step, carry):
        for u in range(UNROLL):
            row = step * UNROLL + u
            out_ref[pl.ds(row, 1), :] = table_ref[pl.ds(idx_ref[row], 1), :]
        return carry

    lax.fori_loop(0, out_ref.shape[0] // UNROLL, body, 0)


def gather_rows(table, idx):
    return pl.pallas_call(
        gather_kernel,
        out_shape=jax.ShapeDtypeStruct((idx.shape[0], table.shape[1]), table.dtype),
        in_specs=[
            pl.BlockSpec(memory_space=pltpu.SMEM),
            pl.BlockSpec(memory_space=pltpu.VMEM),
        ],
        out_specs=pl.BlockSpec(memory_space=pltpu.VMEM),
    )(idx, table)


def split_three(x):
    high = x.astype(jnp.bfloat16)
    rest = x - high.astype(jnp.float32)
    middle = rest.astype(jnp.bfloat16)
    low = (rest - middle.astype(jnp.float32)).astype(jnp.bfloat16)
    return high, middle, low


def bf16_dot(a, b):
    return jnp.dot(a, b, preferred_element_type=jnp.float32)


def three_pass_dot(a, b):
    a_parts, b_parts = split_three(a), split_three(b)
    return bf16_dot(a_parts[0], b_parts[0]) + (
        bf16_dot(a_parts[0], b_parts[1]) + bf16_dot(a_parts[1], b_parts[0])
    )


def fused_kernel(with_send, idx_ref, send_ref, state_ref, halo_ref, mask_ref, pick_ref,
                 spread_ref, folded_ref, out_ref, *rest):
    if with_send:
        sent_ref, table, beside = rest
    else:
        table, beside = rest
    elements = state_ref.shape[0]
    table[0:elements, :] = state_ref[...]
    table[elements:, :] = halo_ref[...]

    def gather(step, carry):
        for u in range(UNROLL):
            row = step * UNROLL + u
            beside[pl.ds(row, 1), :] = table[pl.ds(idx_ref[row], 1), :]
        return carry

    lax.fori_loop(0, beside.shape[0] // UNROLL, gather, 0)
    state = state_ref[...]
    lifted = jnp.zeros_like(state)
    lane_code = lax.broadcasted_iota(jnp.int32, state.shape, 1) // 16
    for face in range(6):
        parts = split_three(beside[face * elements:(face + 1) * elements, :])
        turned = (bf16_dot(parts[0], pick_ref[face]) + bf16_dot(parts[1], pick_ref[face])) + (
            bf16_dot(parts[2], pick_ref[face])
        )
        chosen = jnp.where(mask_ref[face] == lane_code, turned, 0.0)
        lifted = lifted + three_pass_dot(chosen, spread_ref[face])
    own = jnp.dot(
        state, folded_ref[...], precision=lax.Precision.HIGHEST,
        preferred_element_type=jnp.float32,
    )
    rate = own + lifted + state - state * state * state
    out_ref[...] = state + time_step * rate
    if with_send:
        def send(step, carry):
            for u in range(UNROLL):
                row = step * UNROLL + u
                sent_ref[pl.ds(row, 1), :] = out_ref[pl.ds(send_ref[row], 1), :]
            return carry

        lax.fori_loop(0, sent_ref.shape[0] // UNROLL, send, 0)


def fused_step(state, halo, mask, pick, spread, folded, nbr_rows, send_rows, with_send):
    elements, lanes = state.shape
    block = jax.ShapeDtypeStruct((elements, lanes), state.dtype)
    shapes = [block]
    if with_send:
        shapes.append(jax.ShapeDtypeStruct((send_rows.shape[0], lanes), state.dtype))
    vmem = pl.BlockSpec(memory_space=pltpu.VMEM)
    smem = pl.BlockSpec(memory_space=pltpu.SMEM)
    flops = 2 * 6 * 6 * elements * lanes * (2 * lanes) + 2 * 6 * elements * lanes * lanes
    moved = 4 * (4 * elements * lanes + mask.size + pick.size + spread.size)
    result = pl.pallas_call(
        functools.partial(fused_kernel, with_send),
        out_shape=tuple(shapes),
        in_specs=[smem, smem] + [vmem] * 6,
        out_specs=tuple([vmem] * len(shapes)),
        scratch_shapes=[
            pltpu.VMEM((elements + halo.shape[0], lanes), jnp.float32),
            pltpu.VMEM((nbr_rows.shape[0], lanes), jnp.float32),
        ],
        cost_estimate=pl.CostEstimate(flops=flops, transcendentals=0, bytes_accessed=moved),
    )(nbr_rows, send_rows, state, halo, mask, pick, spread, folded)
    return result


def shards(start_state, stiffness, lifting, coarse, neighbor, orientation, send_low, send_high):
    pick_np, own_np = selection_tables()
    pick = jnp.asarray(pick_np, dtype=jnp.bfloat16)
    own = jnp.asarray(own_np)
    lift_t = lifting.T.reshape(6, 16, 64)
    spread = jnp.broadcast_to(lift_t[:, None], (6, 8, 16, 64)).reshape(6, LANES, 64)
    folded = stiffness.T - product(own, lifting.T)
    mask = orientation[:, :, None]
    nbr_rows = neighbor.reshape(-1)
    send_rows = jnp.concatenate([send_low, send_high])
    spread = jnp.pad(spread, ((0, 0), (0, 0), (0, LANES - 64)))
    folded = jnp.pad(folded, ((0, LANES - 64), (0, LANES - 64)))

    state_start = start_state[0]
    state = jnp.pad(state_start.T, ((0, 0), (0, LANES - state_start.shape[0])))
    sent = gather_rows(state, send_rows)
    half = send_low.shape[0]
    for step_id in range(STEPS):
        before = ring(sent[half:, 48:64].T, "space", 1)
        after = ring(sent[:half, 0:16].T, "space", -1)
        halo = jnp.concatenate(
            [
                jnp.pad(before.T, ((0, 0), (48, LANES - 64))),
                jnp.pad(after.T, ((0, 0), (0, LANES - 16))),
            ],
            axis=0,
        )
        with_send = step_id < STEPS - 1
        result = fused_step(
            state, halo, mask, pick, spread, folded, nbr_rows, send_rows, with_send
        )
        state = result[0]
        if with_send:
            sent = result[1]
    fine_state = state[:, : state_start.shape[0]].T
    coarse_start = product(coarse, state_start)
    defect = fine_state - coarse_start
    is_first = lax.axis_index("tm") == 0
    total = jnp.where(is_first, coarse_start + defect, defect)
    return scan_over_time(total, coarse)[None]


def scan_over_time(total, coarse):
    peers = lax.axis_size("tm")
    core = lax.axis_index("tm") % 2
    partner = [(i, i ^ 1) for i in range(peers)]
    half = total.shape[1] // 2
    low, high = total[:, :half], total[:, half:]
    got = lax.ppermute(jnp.where(core == 0, high, low), "tm", partner)
    keep = jnp.where(core == 0, low, high)
    first = jnp.where(core == 0, keep, got)
    second = jnp.where(core == 0, got, keep)
    aggregate = product(coarse, first) + second
    square = product(coarse, coarse)
    before = from_behind(aggregate, "tm", 2)
    power = square
    shift = 1
    while shift < peers // 2:
        before = before + product(power, from_behind(before, "tm", 2 * shift))
        shift *= 2
        if shift < peers // 2:
            power = product(power, power)
    end_first = product(coarse, before) + first
    end_second = product(square, before) + aggregate
    mine = jnp.where(core == 0, end_first, end_second)
    got = lax.ppermute(jnp.where(core == 0, end_second, end_first), "tm", partner)
    return jnp.where(
        core == 0,
        jnp.concatenate([mine, got], axis=1),
        jnp.concatenate([got, mine], axis=1),
    )


def solution(mesh):
    return jax.shard_map(
        shards,
        mesh=mesh,
        in_specs=(
            P("tm", None, "space"),
            P(),
            P(),
            P(),
            P(None, "space"),
            P(None, "space"),
            P("space"),
            P("space"),
        ),
        out_specs=P("tm", None, "space"),
        check_vma=False,
    )
```

```python
import functools

import numpy as np
import jax
import jax.numpy as jnp
from jax import lax
from jax.experimental import pallas as pl
from jax.experimental.pallas import tpu as pltpu
from jax.sharding import PartitionSpec as P

STEPS = 3
LANES = 128
UNROLL = 64


time_step = 0.05


def from_behind(shard, axis, by):
    peers = lax.axis_size(axis)
    pairs = [(i, i + by) for i in range(peers) if 0 <= i + by < peers]
    return lax.ppermute(shard, axis, pairs)


def ring(shard, axis, by):
    peers = lax.axis_size(axis)
    return lax.ppermute(shard, axis, [(i, (i + by) % peers) for i in range(peers)])


def product(matrix, vector):
    return jnp.dot(
        matrix, vector, precision=lax.Precision.HIGHEST, preferred_element_type=jnp.float32
    )


def face_nodes():
    i, j, k = np.meshgrid(np.arange(4), np.arange(4), np.arange(4), indexing="ij")
    node = 16 * i + 4 * j + k
    return [
        node[0].ravel(), node[3].ravel(),
        node[:, 0].ravel(), node[:, 3].ravel(),
        node[:, :, 0].ravel(), node[:, :, 3].ravel(),
    ]


def orientations():
    base = np.arange(16).reshape(4, 4)
    out = []
    for code in range(8):
        turned = base
        if code & 4:
            turned = turned.T
        if code & 1:
            turned = turned[::-1]
        if code & 2:
            turned = turned[:, ::-1]
        out.append(turned.ravel())
    return out


def selection_tables():
    nodes, perms = face_nodes(), orientations()
    pick = np.zeros((6, LANES, LANES), np.float32)
    own = np.zeros((64, 96), np.float32)
    for f in range(6):
        for code in range(8):
            for q in range(16):
                pick[f, nodes[f ^ 1][perms[code][q]], 16 * code + q] = 1.0
        for m in range(16):
            own[nodes[f][m], 16 * f + m] = 1.0
    return pick, own


def gather_kernel(idx_ref, table_ref, out_ref):
    def body(step, carry):
        for u in range(UNROLL):
            row = step * UNROLL + u
            out_ref[pl.ds(row, 1), :] = table_ref[pl.ds(idx_ref[row], 1), :]
        return carry

    lax.fori_loop(0, out_ref.shape[0] // UNROLL, body, 0)


def gather_rows(table, idx):
    return pl.pallas_call(
        gather_kernel,
        out_shape=jax.ShapeDtypeStruct((idx.shape[0], table.shape[1]), table.dtype),
        in_specs=[
            pl.BlockSpec(memory_space=pltpu.SMEM),
            pl.BlockSpec(memory_space=pltpu.VMEM),
        ],
        out_specs=pl.BlockSpec(memory_space=pltpu.VMEM),
    )(idx, table)


def split_three(x):
    high = x.astype(jnp.bfloat16)
    rest = x - high.astype(jnp.float32)
    middle = rest.astype(jnp.bfloat16)
    low = (rest - middle.astype(jnp.float32)).astype(jnp.bfloat16)
    return high, middle, low


def bf16_dot(a, b):
    return jnp.dot(a, b, preferred_element_type=jnp.float32)


def three_pass_dot(a, b):
    a_parts, b_parts = split_three(a), split_three(b)
    return bf16_dot(a_parts[0], b_parts[0]) + (
        bf16_dot(a_parts[0], b_parts[1]) + bf16_dot(a_parts[1], b_parts[0])
    )


def fused_kernel(with_send, idx_ref, send_ref, state_ref, halo_ref, mask_ref, pick_ref,
                 spread_ref, folded_ref, out_ref, *rest):
    if with_send:
        sent_ref, table, beside = rest
    else:
        table, beside = rest
    elements = state_ref.shape[0]
    table[0:elements, :] = state_ref[...]
    table[elements:, :] = halo_ref[...]

    def gather(step, carry):
        for u in range(UNROLL):
            row = step * UNROLL + u
            beside[pl.ds(row, 1), :] = table[pl.ds(idx_ref[row], 1), :]
        return carry

    lax.fori_loop(0, beside.shape[0] // UNROLL, gather, 0)
    state = state_ref[...]
    lifted = jnp.zeros_like(state)
    lane_code = lax.broadcasted_iota(jnp.int32, state.shape, 1) // 16
    for face in range(6):
        parts = split_three(beside[face * elements:(face + 1) * elements, :])
        turned = (bf16_dot(parts[0], pick_ref[face]) + bf16_dot(parts[1], pick_ref[face])) + (
            bf16_dot(parts[2], pick_ref[face])
        )
        chosen = jnp.where(mask_ref[face] == lane_code, turned, 0.0)
        lifted = lifted + three_pass_dot(chosen, spread_ref[face])
    own = three_pass_dot(state, folded_ref[...])
    rate = own + lifted + state - state * state * state
    out_ref[...] = state + time_step * rate
    if with_send:
        def send(step, carry):
            for u in range(UNROLL):
                row = step * UNROLL + u
                sent_ref[pl.ds(row, 1), :] = out_ref[pl.ds(send_ref[row], 1), :]
            return carry

        lax.fori_loop(0, sent_ref.shape[0] // UNROLL, send, 0)


def fused_step(state, halo, mask, pick, spread, folded, nbr_rows, send_rows, with_send):
    elements, lanes = state.shape
    block = jax.ShapeDtypeStruct((elements, lanes), state.dtype)
    shapes = [block]
    if with_send:
        shapes.append(jax.ShapeDtypeStruct((send_rows.shape[0], lanes), state.dtype))
    vmem = pl.BlockSpec(memory_space=pltpu.VMEM)
    smem = pl.BlockSpec(memory_space=pltpu.SMEM)
    flops = 2 * 6 * 6 * elements * lanes * (2 * lanes) + 2 * 6 * elements * lanes * lanes
    moved = 4 * (4 * elements * lanes + mask.size + pick.size + spread.size)
    result = pl.pallas_call(
        functools.partial(fused_kernel, with_send),
        out_shape=tuple(shapes),
        in_specs=[smem, smem] + [vmem] * 6,
        out_specs=tuple([vmem] * len(shapes)),
        scratch_shapes=[
            pltpu.VMEM((elements + halo.shape[0], lanes), jnp.float32),
            pltpu.VMEM((nbr_rows.shape[0], lanes), jnp.float32),
        ],
        cost_estimate=pl.CostEstimate(flops=flops, transcendentals=0, bytes_accessed=moved),
    )(nbr_rows, send_rows, state, halo, mask, pick, spread, folded)
    return result


def shards(start_state, stiffness, lifting, coarse, neighbor, orientation, send_low, send_high):
    pick_np, own_np = selection_tables()
    pick = jnp.asarray(pick_np, dtype=jnp.bfloat16)
    own = jnp.asarray(own_np)
    lift_t = lifting.T.reshape(6, 16, 64)
    spread = jnp.broadcast_to(lift_t[:, None], (6, 8, 16, 64)).reshape(6, LANES, 64)
    folded = stiffness.T - product(own, lifting.T)
    mask = orientation[:, :, None]
    nbr_rows = neighbor.reshape(-1)
    send_rows = jnp.concatenate([send_low, send_high])
    spread = jnp.pad(spread, ((0, 0), (0, 0), (0, LANES - 64)))
    folded = jnp.pad(folded, ((0, LANES - 64), (0, LANES - 64)))

    state_start = start_state[0]
    state = jnp.pad(state_start.T, ((0, 0), (0, LANES - state_start.shape[0])))
    sent = gather_rows(state, send_rows)
    half = send_low.shape[0]
    for step_id in range(STEPS):
        before = ring(sent[half:, 48:64].T, "space", 1)
        after = ring(sent[:half, 0:16].T, "space", -1)
        halo = jnp.concatenate(
            [
                jnp.pad(before.T, ((0, 0), (48, LANES - 64))),
                jnp.pad(after.T, ((0, 0), (0, LANES - 16))),
            ],
            axis=0,
        )
        with_send = step_id < STEPS - 1
        result = fused_step(
            state, halo, mask, pick, spread, folded, nbr_rows, send_rows, with_send
        )
        state = result[0]
        if with_send:
            sent = result[1]
    fine_state = state[:, : state_start.shape[0]].T
    coarse_start = product(coarse, state_start)
    defect = fine_state - coarse_start
    is_first = lax.axis_index("tm") == 0
    total = jnp.where(is_first, coarse_start + defect, defect)
    return scan_over_time(total, coarse)[None]


def scan_over_time(total, coarse):
    peers = lax.axis_size("tm")
    core = lax.axis_index("tm") % 2
    partner = [(i, i ^ 1) for i in range(peers)]
    half = total.shape[1] // 2
    low, high = total[:, :half], total[:, half:]
    got = lax.ppermute(jnp.where(core == 0, high, low), "tm", partner)
    keep = jnp.where(core == 0, low, high)
    first = jnp.where(core == 0, keep, got)
    second = jnp.where(core == 0, got, keep)
    aggregate = product(coarse, first) + second
    square = product(coarse, coarse)
    before = from_behind(aggregate, "tm", 2)
    power = square
    shift = 1
    while shift < peers // 2:
        before = before + product(power, from_behind(before, "tm", 2 * shift))
        shift *= 2
        if shift < peers // 2:
            power = product(power, power)
    end_first = product(coarse, before) + first
    end_second = product(square, before) + aggregate
    mine = jnp.where(core == 0, end_first, end_second)
    got = lax.ppermute(jnp.where(core == 0, end_second, end_first), "tm", partner)
    return jnp.where(
        core == 0,
        jnp.concatenate([mine, got], axis=1),
        jnp.concatenate([got, mine], axis=1),
    )


def solution(mesh):
    return jax.shard_map(
        shards,
        mesh=mesh,
        in_specs=(
            P("tm", None, "space"),
            P(),
            P(),
            P(),
            P(None, "space"),
            P(None, "space"),
            P("space"),
            P("space"),
        ),
        out_specs=P("tm", None, "space"),
        check_vma=False,
    )
```

```python
import functools

import numpy as np
import jax
import jax.numpy as jnp
from jax import lax
from jax.experimental import pallas as pl
from jax.experimental.pallas import tpu as pltpu
from jax.sharding import PartitionSpec as P

STEPS = 3
LANES = 128
UNROLL = 128


time_step = 0.05


def from_behind(shard, axis, by):
    peers = lax.axis_size(axis)
    pairs = [(i, i + by) for i in range(peers) if 0 <= i + by < peers]
    return lax.ppermute(shard, axis, pairs)


def ring(shard, axis, by):
    peers = lax.axis_size(axis)
    return lax.ppermute(shard, axis, [(i, (i + by) % peers) for i in range(peers)])


def product(matrix, vector):
    return jnp.dot(
        matrix, vector, precision=lax.Precision.HIGHEST, preferred_element_type=jnp.float32
    )


def quick_product(matrix, vector):
    return jnp.dot(
        matrix, vector, precision=lax.Precision.HIGH, preferred_element_type=jnp.float32
    )


def face_nodes():
    i, j, k = np.meshgrid(np.arange(4), np.arange(4), np.arange(4), indexing="ij")
    node = 16 * i + 4 * j + k
    return [
        node[0].ravel(), node[3].ravel(),
        node[:, 0].ravel(), node[:, 3].ravel(),
        node[:, :, 0].ravel(), node[:, :, 3].ravel(),
    ]


def orientations():
    base = np.arange(16).reshape(4, 4)
    out = []
    for code in range(8):
        turned = base
        if code & 4:
            turned = turned.T
        if code & 1:
            turned = turned[::-1]
        if code & 2:
            turned = turned[:, ::-1]
        out.append(turned.ravel())
    return out


def selection_tables():
    nodes, perms = face_nodes(), orientations()
    pick = np.zeros((6, LANES, LANES), np.float32)
    own = np.zeros((64, 96), np.float32)
    for f in range(6):
        for code in range(8):
            for q in range(16):
                pick[f, nodes[f ^ 1][perms[code][q]], 16 * code + q] = 1.0
        for m in range(16):
            own[nodes[f][m], 16 * f + m] = 1.0
    return pick, own


def gather_kernel(idx_ref, table_ref, out_ref):
    def body(step, carry):
        for u in range(UNROLL):
            row = step * UNROLL + u
            out_ref[pl.ds(row, 1), :] = table_ref[pl.ds(idx_ref[row], 1), :]
        return carry

    lax.fori_loop(0, out_ref.shape[0] // UNROLL, body, 0)


def gather_rows(table, idx):
    return pl.pallas_call(
        gather_kernel,
        out_shape=jax.ShapeDtypeStruct((idx.shape[0], table.shape[1]), table.dtype),
        in_specs=[
            pl.BlockSpec(memory_space=pltpu.SMEM),
            pl.BlockSpec(memory_space=pltpu.VMEM),
        ],
        out_specs=pl.BlockSpec(memory_space=pltpu.VMEM),
    )(idx, table)


def split_three(x):
    high = x.astype(jnp.bfloat16)
    rest = x - high.astype(jnp.float32)
    middle = rest.astype(jnp.bfloat16)
    low = (rest - middle.astype(jnp.float32)).astype(jnp.bfloat16)
    return high, middle, low


def bf16_dot(a, b):
    return jnp.dot(a, b, preferred_element_type=jnp.float32)


def three_pass_dot(a, b):
    a_parts, b_parts = split_three(a), split_three(b)
    return bf16_dot(a_parts[0], b_parts[0]) + (
        bf16_dot(a_parts[0], b_parts[1]) + bf16_dot(a_parts[1], b_parts[0])
    )


def fused_kernel(with_send, idx_ref, send_ref, state_ref, halo_ref, mask_ref, pick_ref,
                 spread_ref, folded_ref, out_ref, *rest):
    if with_send:
        sent_ref, table, beside = rest
    else:
        table, beside = rest
    elements = state_ref.shape[0]
    table[0:elements, :] = state_ref[...]
    table[elements:, :] = halo_ref[...]

    def gather(step, carry):
        for u in range(UNROLL):
            row = step * UNROLL + u
            beside[pl.ds(row, 1), :] = table[pl.ds(idx_ref[row], 1), :]
        return carry

    lax.fori_loop(0, beside.shape[0] // UNROLL, gather, 0)
    state = state_ref[...]
    lifted = jnp.zeros_like(state)
    lane_code = lax.broadcasted_iota(jnp.int32, state.shape, 1) // 16
    for face in range(6):
        parts = split_three(beside[face * elements:(face + 1) * elements, :])
        turned = (bf16_dot(parts[0], pick_ref[face]) + bf16_dot(parts[1], pick_ref[face])) + (
            bf16_dot(parts[2], pick_ref[face])
        )
        chosen = jnp.where(mask_ref[face] == lane_code, turned, 0.0)
        lifted = lifted + three_pass_dot(chosen, spread_ref[face])
    own = three_pass_dot(state, folded_ref[...])
    rate = own + lifted + state - state * state * state
    out_ref[...] = state + time_step * rate
    if with_send:
        def send(step, carry):
            for u in range(UNROLL):
                row = step * UNROLL + u
                sent_ref[pl.ds(row, 1), :] = out_ref[pl.ds(send_ref[row], 1), :]
            return carry

        lax.fori_loop(0, sent_ref.shape[0] // UNROLL, send, 0)


def fused_step(state, halo, mask, pick, spread, folded, nbr_rows, send_rows, with_send):
    elements, lanes = state.shape
    block = jax.ShapeDtypeStruct((elements, lanes), state.dtype)
    shapes = [block]
    if with_send:
        shapes.append(jax.ShapeDtypeStruct((send_rows.shape[0], lanes), state.dtype))
    vmem = pl.BlockSpec(memory_space=pltpu.VMEM)
    smem = pl.BlockSpec(memory_space=pltpu.SMEM)
    flops = 2 * 6 * 6 * elements * lanes * (2 * lanes) + 2 * 6 * elements * lanes * lanes
    moved = 4 * (4 * elements * lanes + mask.size + pick.size + spread.size)
    result = pl.pallas_call(
        functools.partial(fused_kernel, with_send),
        out_shape=tuple(shapes),
        in_specs=[smem, smem] + [vmem] * 6,
        out_specs=tuple([vmem] * len(shapes)),
        scratch_shapes=[
            pltpu.VMEM((elements + halo.shape[0], lanes), jnp.float32),
            pltpu.VMEM((nbr_rows.shape[0], lanes), jnp.float32),
        ],
        cost_estimate=pl.CostEstimate(flops=flops, transcendentals=0, bytes_accessed=moved),
    )(nbr_rows, send_rows, state, halo, mask, pick, spread, folded)
    return result


def shards(start_state, stiffness, lifting, coarse, neighbor, orientation, send_low, send_high):
    pick_np, own_np = selection_tables()
    pick = jnp.asarray(pick_np, dtype=jnp.bfloat16)
    own = jnp.asarray(own_np)
    lift_t = lifting.T.reshape(6, 16, 64)
    spread = jnp.broadcast_to(lift_t[:, None], (6, 8, 16, 64)).reshape(6, LANES, 64)
    folded = stiffness.T - product(own, lifting.T)
    mask = orientation[:, :, None]
    nbr_rows = neighbor.reshape(-1)
    send_rows = jnp.concatenate([send_low, send_high])
    spread = jnp.pad(spread, ((0, 0), (0, 0), (0, LANES - 64)))
    folded = jnp.pad(folded, ((0, LANES - 64), (0, LANES - 64)))

    state_start = start_state[0]
    state = jnp.pad(state_start.T, ((0, 0), (0, LANES - state_start.shape[0])))
    sent = gather_rows(state, send_rows)
    half = send_low.shape[0]
    for step_id in range(STEPS):
        before = ring(sent[half:, 48:64].T, "space", 1)
        after = ring(sent[:half, 0:16].T, "space", -1)
        halo = jnp.concatenate(
            [
                jnp.pad(before.T, ((0, 0), (48, LANES - 64))),
                jnp.pad(after.T, ((0, 0), (0, LANES - 16))),
            ],
            axis=0,
        )
        with_send = step_id < STEPS - 1
        result = fused_step(
            state, halo, mask, pick, spread, folded, nbr_rows, send_rows, with_send
        )
        state = result[0]
        if with_send:
            sent = result[1]
    fine_state = state[:, : state_start.shape[0]].T
    coarse_start = product(coarse, state_start)
    defect = fine_state - coarse_start
    is_first = lax.axis_index("tm") == 0
    total = jnp.where(is_first, coarse_start + defect, defect)
    return scan_over_time(total, coarse)[None]


def scan_over_time(total, coarse):
    peers = lax.axis_size("tm")
    core = lax.axis_index("tm") % 2
    partner = [(i, i ^ 1) for i in range(peers)]
    half = total.shape[1] // 2
    low, high = total[:, :half], total[:, half:]
    got = lax.ppermute(jnp.where(core == 0, high, low), "tm", partner)
    keep = jnp.where(core == 0, low, high)
    first = jnp.where(core == 0, keep, got)
    second = jnp.where(core == 0, got, keep)
    aggregate = quick_product(coarse, first) + second
    square = product(coarse, coarse)
    before = from_behind(aggregate, "tm", 2)
    power = square
    shift = 1
    while shift < peers // 2:
        before = before + quick_product(power, from_behind(before, "tm", 2 * shift))
        shift *= 2
        if shift < peers // 2:
            power = product(power, power)
    end_first = quick_product(coarse, before) + first
    end_second = quick_product(square, before) + aggregate
    mine = jnp.where(core == 0, end_first, end_second)
    got = lax.ppermute(jnp.where(core == 0, end_second, end_first), "tm", partner)
    return jnp.where(
        core == 0,
        jnp.concatenate([mine, got], axis=1),
        jnp.concatenate([got, mine], axis=1),
    )


def solution(mesh):
    return jax.shard_map(
        shards,
        mesh=mesh,
        in_specs=(
            P("tm", None, "space"),
            P(),
            P(),
            P(),
            P(None, "space"),
            P(None, "space"),
            P("space"),
            P("space"),
        ),
        out_specs=P("tm", None, "space"),
        check_vma=False,
    )
```

```python
import functools

import numpy as np
import jax
import jax.numpy as jnp
from jax import lax
from jax.experimental import pallas as pl
from jax.experimental.pallas import tpu as pltpu
from jax.sharding import PartitionSpec as P

STEPS = 3
LANES = 128
UNROLL = 128


time_step = 0.05


def from_behind(shard, axis, by):
    peers = lax.axis_size(axis)
    pairs = [(i, i + by) for i in range(peers) if 0 <= i + by < peers]
    return lax.ppermute(shard, axis, pairs)


def ring(shard, axis, by):
    peers = lax.axis_size(axis)
    return lax.ppermute(shard, axis, [(i, (i + by) % peers) for i in range(peers)])


def product(matrix, vector):
    return jnp.dot(
        matrix, vector, precision=lax.Precision.HIGHEST, preferred_element_type=jnp.float32
    )


def face_nodes():
    i, j, k = np.meshgrid(np.arange(4), np.arange(4), np.arange(4), indexing="ij")
    node = 16 * i + 4 * j + k
    return [
        node[0].ravel(), node[3].ravel(),
        node[:, 0].ravel(), node[:, 3].ravel(),
        node[:, :, 0].ravel(), node[:, :, 3].ravel(),
    ]


def orientations():
    base = np.arange(16).reshape(4, 4)
    out = []
    for code in range(8):
        turned = base
        if code & 4:
            turned = turned.T
        if code & 1:
            turned = turned[::-1]
        if code & 2:
            turned = turned[:, ::-1]
        out.append(turned.ravel())
    return out


def selection_tables():
    nodes, perms = face_nodes(), orientations()
    pick = np.zeros((6, LANES, LANES), np.float32)
    own = np.zeros((64, 96), np.float32)
    for f in range(6):
        for code in range(8):
            for q in range(16):
                pick[f, nodes[f ^ 1][perms[code][q]], 16 * code + q] = 1.0
        for m in range(16):
            own[nodes[f][m], 16 * f + m] = 1.0
    return pick, own


def gather_kernel(idx_ref, table_ref, out_ref):
    def body(step, carry):
        for u in range(UNROLL):
            row = step * UNROLL + u
            out_ref[pl.ds(row, 1), :] = table_ref[pl.ds(idx_ref[row], 1), :]
        return carry

    lax.fori_loop(0, out_ref.shape[0] // UNROLL, body, 0)


def gather_rows(table, idx):
    return pl.pallas_call(
        gather_kernel,
        out_shape=jax.ShapeDtypeStruct((idx.shape[0], table.shape[1]), table.dtype),
        in_specs=[
            pl.BlockSpec(memory_space=pltpu.SMEM),
            pl.BlockSpec(memory_space=pltpu.VMEM),
        ],
        out_specs=pl.BlockSpec(memory_space=pltpu.VMEM),
    )(idx, table)


def split_three(x):
    high = x.astype(jnp.bfloat16)
    rest = x - high.astype(jnp.float32)
    middle = rest.astype(jnp.bfloat16)
    low = (rest - middle.astype(jnp.float32)).astype(jnp.bfloat16)
    return high, middle, low


def bf16_dot(a, b):
    return jnp.dot(a, b, preferred_element_type=jnp.float32)


def three_pass_dot(a, b):
    a_parts, b_parts = split_three(a), split_three(b)
    return bf16_dot(a_parts[0], b_parts[0]) + (
        bf16_dot(a_parts[0], b_parts[1]) + bf16_dot(a_parts[1], b_parts[0])
    )


def fused_kernel(with_send, idx_ref, send_ref, state_ref, halo_ref, mask_ref, pick_ref,
                 spread_ref, folded_ref, out_ref, *rest):
    if with_send:
        sent_ref, table, beside = rest
    else:
        table, beside = rest
    elements = state_ref.shape[0]
    table[0:elements, :] = state_ref[...]
    table[elements:, :] = halo_ref[...]

    def gather(step, carry):
        for u in range(UNROLL):
            row = step * UNROLL + u
            beside[pl.ds(row, 1), :] = table[pl.ds(idx_ref[row], 1), :]
        return carry

    lax.fori_loop(0, beside.shape[0] // UNROLL, gather, 0)
    state = state_ref[...]
    lifted = jnp.zeros_like(state)
    lane_code = lax.broadcasted_iota(jnp.int32, state.shape, 1) // 16
    for face in range(6):
        parts = split_three(beside[face * elements:(face + 1) * elements, :])
        turned = (bf16_dot(parts[0], pick_ref[face]) + bf16_dot(parts[1], pick_ref[face])) + (
            bf16_dot(parts[2], pick_ref[face])
        )
        chosen = jnp.where(mask_ref[face] == lane_code, turned, 0.0)
        lifted = lifted + three_pass_dot(chosen, spread_ref[face])
    own = three_pass_dot(state, folded_ref[...])
    rate = own + lifted + state - state * state * state
    out_ref[...] = state + time_step * rate
    if with_send:
        def send(step, carry):
            for u in range(UNROLL):
                row = step * UNROLL + u
                sent_ref[pl.ds(row, 1), :] = out_ref[pl.ds(send_ref[row], 1), :]
            return carry

        lax.fori_loop(0, sent_ref.shape[0] // UNROLL, send, 0)


def fused_step(state, halo, mask, pick, spread, folded, nbr_rows, send_rows, with_send):
    elements, lanes = state.shape
    block = jax.ShapeDtypeStruct((elements, lanes), state.dtype)
    shapes = [block]
    if with_send:
        shapes.append(jax.ShapeDtypeStruct((send_rows.shape[0], lanes), state.dtype))
    vmem = pl.BlockSpec(memory_space=pltpu.VMEM)
    smem = pl.BlockSpec(memory_space=pltpu.SMEM)
    flops = 2 * 6 * 6 * elements * lanes * (2 * lanes) + 2 * 6 * elements * lanes * lanes
    moved = 4 * (4 * elements * lanes + mask.size + pick.size + spread.size)
    result = pl.pallas_call(
        functools.partial(fused_kernel, with_send),
        out_shape=tuple(shapes),
        in_specs=[smem, smem] + [vmem] * 6,
        out_specs=tuple([vmem] * len(shapes)),
        scratch_shapes=[
            pltpu.VMEM((elements + halo.shape[0], lanes), jnp.float32),
            pltpu.VMEM((nbr_rows.shape[0], lanes), jnp.float32),
        ],
        cost_estimate=pl.CostEstimate(flops=flops, transcendentals=0, bytes_accessed=moved),
    )(nbr_rows, send_rows, state, halo, mask, pick, spread, folded)
    return result


def shards(start_state, stiffness, lifting, coarse, neighbor, orientation, send_low, send_high):
    pick_np, own_np = selection_tables()
    pick = jnp.asarray(pick_np, dtype=jnp.bfloat16)
    own = jnp.asarray(own_np)
    lift_t = lifting.T.reshape(6, 16, 64)
    spread = jnp.broadcast_to(lift_t[:, None], (6, 8, 16, 64)).reshape(6, LANES, 64)
    folded = stiffness.T - product(own, lifting.T)
    mask = orientation[:, :, None]
    nbr_rows = neighbor.reshape(-1)
    send_rows = jnp.concatenate([send_low, send_high])
    spread = jnp.pad(spread, ((0, 0), (0, 0), (0, LANES - 64)))
    folded = jnp.pad(folded, ((0, LANES - 64), (0, LANES - 64)))

    state_start = start_state[0]
    state = jnp.pad(state_start.T, ((0, 0), (0, LANES - state_start.shape[0])))
    sent = gather_rows(state, send_rows)
    half = send_low.shape[0]
    for step_id in range(STEPS):
        before = ring(sent[half:, 48:64].T, "space", 1)
        after = ring(sent[:half, 0:16].T, "space", -1)
        halo = jnp.concatenate(
            [
                jnp.pad(before.T, ((0, 0), (48, LANES - 64))),
                jnp.pad(after.T, ((0, 0), (0, LANES - 16))),
            ],
            axis=0,
        )
        with_send = step_id < STEPS - 1
        result = fused_step(
            state, halo, mask, pick, spread, folded, nbr_rows, send_rows, with_send
        )
        state = result[0]
        if with_send:
            sent = result[1]
    fine_state = state[:, : state_start.shape[0]].T
    coarse_start = product(coarse, state_start)
    defect = fine_state - coarse_start
    is_first = lax.axis_index("tm") == 0
    total = jnp.where(is_first, coarse_start + defect, defect)
    return scan_over_time(total, coarse)[None]


def scan_over_time(total, coarse):
    peers = lax.axis_size("tm")
    core = lax.axis_index("tm") % 2
    partner = [(i, i ^ 1) for i in range(peers)]
    half = total.shape[1] // 2
    low, high = total[:, :half], total[:, half:]
    got = lax.ppermute(jnp.where(core == 0, high, low), "tm", partner)
    keep = jnp.where(core == 0, low, high)
    first = jnp.where(core == 0, keep, got)
    second = jnp.where(core == 0, got, keep)
    aggregate = product(coarse, first) + second
    square = product(coarse, coarse)
    before = from_behind(aggregate, "tm", 2)
    power = square
    shift = 1
    while shift < peers // 2:
        before = before + product(power, from_behind(before, "tm", 2 * shift))
        shift *= 2
        if shift < peers // 2:
            power = product(power, power)
    end_first = product(coarse, before) + first
    end_second = product(square, before) + aggregate
    mine = jnp.where(core == 0, end_first, end_second)
    got = lax.ppermute(jnp.where(core == 0, end_second, end_first), "tm", partner)
    return jnp.where(
        core == 0,
        jnp.concatenate([mine, got], axis=1),
        jnp.concatenate([got, mine], axis=1),
    )


def solution(mesh):
    return jax.shard_map(
        shards,
        mesh=mesh,
        in_specs=(
            P("tm", None, "space"),
            P(),
            P(),
            P(),
            P(None, "space"),
            P(None, "space"),
            P("space"),
            P("space"),
        ),
        out_specs=P("tm", None, "space"),
        check_vma=False,
    )
```

```python
import functools

import numpy as np
import jax
import jax.numpy as jnp
from jax import lax
from jax.experimental import pallas as pl
from jax.experimental.pallas import tpu as pltpu
from jax.sharding import PartitionSpec as P

STEPS = 3
LANES = 128
UNROLL = 256


time_step = 0.05


def from_behind(shard, axis, by):
    peers = lax.axis_size(axis)
    pairs = [(i, i + by) for i in range(peers) if 0 <= i + by < peers]
    return lax.ppermute(shard, axis, pairs)


def ring(shard, axis, by):
    peers = lax.axis_size(axis)
    return lax.ppermute(shard, axis, [(i, (i + by) % peers) for i in range(peers)])


def product(matrix, vector):
    return jnp.dot(
        matrix, vector, precision=lax.Precision.HIGHEST, preferred_element_type=jnp.float32
    )


def face_nodes():
    i, j, k = np.meshgrid(np.arange(4), np.arange(4), np.arange(4), indexing="ij")
    node = 16 * i + 4 * j + k
    return [
        node[0].ravel(), node[3].ravel(),
        node[:, 0].ravel(), node[:, 3].ravel(),
        node[:, :, 0].ravel(), node[:, :, 3].ravel(),
    ]


def orientations():
    base = np.arange(16).reshape(4, 4)
    out = []
    for code in range(8):
        turned = base
        if code & 4:
            turned = turned.T
        if code & 1:
            turned = turned[::-1]
        if code & 2:
            turned = turned[:, ::-1]
        out.append(turned.ravel())
    return out


def selection_tables():
    nodes, perms = face_nodes(), orientations()
    pick = np.zeros((6, LANES, LANES), np.float32)
    own = np.zeros((64, 96), np.float32)
    for f in range(6):
        for code in range(8):
            for q in range(16):
                pick[f, nodes[f ^ 1][perms[code][q]], 16 * code + q] = 1.0
        for m in range(16):
            own[nodes[f][m], 16 * f + m] = 1.0
    return pick, own


def gather_kernel(idx_ref, table_ref, out_ref):
    def body(step, carry):
        for u in range(UNROLL):
            row = step * UNROLL + u
            out_ref[pl.ds(row, 1), :] = table_ref[pl.ds(idx_ref[row], 1), :]
        return carry

    lax.fori_loop(0, out_ref.shape[0] // UNROLL, body, 0)


def gather_rows(table, idx):
    return pl.pallas_call(
        gather_kernel,
        out_shape=jax.ShapeDtypeStruct((idx.shape[0], table.shape[1]), table.dtype),
        in_specs=[
            pl.BlockSpec(memory_space=pltpu.SMEM),
            pl.BlockSpec(memory_space=pltpu.VMEM),
        ],
        out_specs=pl.BlockSpec(memory_space=pltpu.VMEM),
    )(idx, table)


def split_three(x):
    high = x.astype(jnp.bfloat16)
    rest = x - high.astype(jnp.float32)
    middle = rest.astype(jnp.bfloat16)
    low = (rest - middle.astype(jnp.float32)).astype(jnp.bfloat16)
    return high, middle, low


def bf16_dot(a, b):
    return jnp.dot(a, b, preferred_element_type=jnp.float32)


def three_pass_dot(a, b):
    a_parts, b_parts = split_three(a), split_three(b)
    return bf16_dot(a_parts[0], b_parts[0]) + (
        bf16_dot(a_parts[0], b_parts[1]) + bf16_dot(a_parts[1], b_parts[0])
    )


def fused_kernel(with_send, idx_ref, send_ref, state_ref, halo_ref, mask_ref, pick_ref,
                 spread_ref, folded_ref, out_ref, *rest):
    if with_send:
        sent_ref, table, beside = rest
    else:
        table, beside = rest
    elements = state_ref.shape[0]
    table[0:elements, :] = state_ref[...]
    table[elements:, :] = halo_ref[...]

    def gather(step, carry):
        for u in range(UNROLL):
            row = step * UNROLL + u
            beside[pl.ds(row, 1), :] = table[pl.ds(idx_ref[row], 1), :]
        return carry

    lax.fori_loop(0, beside.shape[0] // UNROLL, gather, 0)
    state = state_ref[...]
    lifted = jnp.zeros_like(state)
    lane_code = lax.broadcasted_iota(jnp.int32, state.shape, 1) // 16
    for face in range(6):
        parts = split_three(beside[face * elements:(face + 1) * elements, :])
        turned = (bf16_dot(parts[0], pick_ref[face]) + bf16_dot(parts[1], pick_ref[face])) + (
            bf16_dot(parts[2], pick_ref[face])
        )
        chosen = jnp.where(mask_ref[face] == lane_code, turned, 0.0)
        lifted = lifted + three_pass_dot(chosen, spread_ref[face])
    own = three_pass_dot(state, folded_ref[...])
    rate = own + lifted + state - state * state * state
    out_ref[...] = state + time_step * rate
    if with_send:
        def send(step, carry):
            for u in range(UNROLL):
                row = step * UNROLL + u
                sent_ref[pl.ds(row, 1), :] = out_ref[pl.ds(send_ref[row], 1), :]
            return carry

        lax.fori_loop(0, sent_ref.shape[0] // UNROLL, send, 0)


def fused_step(state, halo, mask, pick, spread, folded, nbr_rows, send_rows, with_send):
    elements, lanes = state.shape
    block = jax.ShapeDtypeStruct((elements, lanes), state.dtype)
    shapes = [block]
    if with_send:
        shapes.append(jax.ShapeDtypeStruct((send_rows.shape[0], lanes), state.dtype))
    vmem = pl.BlockSpec(memory_space=pltpu.VMEM)
    smem = pl.BlockSpec(memory_space=pltpu.SMEM)
    flops = 2 * 6 * 6 * elements * lanes * (2 * lanes) + 2 * 6 * elements * lanes * lanes
    moved = 4 * (4 * elements * lanes + mask.size + pick.size + spread.size)
    result = pl.pallas_call(
        functools.partial(fused_kernel, with_send),
        out_shape=tuple(shapes),
        in_specs=[smem, smem] + [vmem] * 6,
        out_specs=tuple([vmem] * len(shapes)),
        scratch_shapes=[
            pltpu.VMEM((elements + halo.shape[0], lanes), jnp.float32),
            pltpu.VMEM((nbr_rows.shape[0], lanes), jnp.float32),
        ],
        cost_estimate=pl.CostEstimate(flops=flops, transcendentals=0, bytes_accessed=moved),
    )(nbr_rows, send_rows, state, halo, mask, pick, spread, folded)
    return result


def shards(start_state, stiffness, lifting, coarse, neighbor, orientation, send_low, send_high):
    pick_np, own_np = selection_tables()
    pick = jnp.asarray(pick_np, dtype=jnp.bfloat16)
    own = jnp.asarray(own_np)
    lift_t = lifting.T.reshape(6, 16, 64)
    spread = jnp.broadcast_to(lift_t[:, None], (6, 8, 16, 64)).reshape(6, LANES, 64)
    folded = stiffness.T - product(own, lifting.T)
    mask = orientation[:, :, None]
    nbr_rows = neighbor.reshape(-1)
    send_rows = jnp.concatenate([send_low, send_high])
    spread = jnp.pad(spread, ((0, 0), (0, 0), (0, LANES - 64)))
    folded = jnp.pad(folded, ((0, LANES - 64), (0, LANES - 64)))

    state_start = start_state[0]
    state = jnp.pad(state_start.T, ((0, 0), (0, LANES - state_start.shape[0])))
    sent = gather_rows(state, send_rows)
    half = send_low.shape[0]
    for step_id in range(STEPS):
        before = ring(sent[half:, 48:64].T, "space", 1)
        after = ring(sent[:half, 0:16].T, "space", -1)
        halo = jnp.concatenate(
            [
                jnp.pad(before.T, ((0, 0), (48, LANES - 64))),
                jnp.pad(after.T, ((0, 0), (0, LANES - 16))),
            ],
            axis=0,
        )
        with_send = step_id < STEPS - 1
        result = fused_step(
            state, halo, mask, pick, spread, folded, nbr_rows, send_rows, with_send
        )
        state = result[0]
        if with_send:
            sent = result[1]
    fine_state = state[:, : state_start.shape[0]].T
    coarse_start = product(coarse, state_start)
    defect = fine_state - coarse_start
    is_first = lax.axis_index("tm") == 0
    total = jnp.where(is_first, coarse_start + defect, defect)
    return scan_over_time(total, coarse)[None]


def scan_over_time(total, coarse):
    peers = lax.axis_size("tm")
    core = lax.axis_index("tm") % 2
    partner = [(i, i ^ 1) for i in range(peers)]
    half = total.shape[1] // 2
    low, high = total[:, :half], total[:, half:]
    got = lax.ppermute(jnp.where(core == 0, high, low), "tm", partner)
    keep = jnp.where(core == 0, low, high)
    first = jnp.where(core == 0, keep, got)
    second = jnp.where(core == 0, got, keep)
    aggregate = product(coarse, first) + second
    square = product(coarse, coarse)
    before = from_behind(aggregate, "tm", 2)
    power = square
    shift = 1
    while shift < peers // 2:
        before = before + product(power, from_behind(before, "tm", 2 * shift))
        shift *= 2
        if shift < peers // 2:
            power = product(power, power)
    end_first = product(coarse, before) + first
    end_second = product(square, before) + aggregate
    mine = jnp.where(core == 0, end_first, end_second)
    got = lax.ppermute(jnp.where(core == 0, end_second, end_first), "tm", partner)
    return jnp.where(
        core == 0,
        jnp.concatenate([mine, got], axis=1),
        jnp.concatenate([got, mine], axis=1),
    )


def solution(mesh):
    return jax.shard_map(
        shards,
        mesh=mesh,
        in_specs=(
            P("tm", None, "space"),
            P(),
            P(),
            P(),
            P(None, "space"),
            P(None, "space"),
            P("space"),
            P("space"),
        ),
        out_specs=P("tm", None, "space"),
        check_vma=False,
    )
```

```python
import functools

import numpy as np
import jax
import jax.numpy as jnp
from jax import lax
from jax.experimental import pallas as pl
from jax.experimental.pallas import tpu as pltpu
from jax.sharding import PartitionSpec as P

STEPS = 3
LANES = 128
UNROLL = 256


time_step = 0.05


def from_behind(shard, axis, by):
    peers = lax.axis_size(axis)
    pairs = [(i, i + by) for i in range(peers) if 0 <= i + by < peers]
    return lax.ppermute(shard, axis, pairs)


def ring(shard, axis, by):
    peers = lax.axis_size(axis)
    return lax.ppermute(shard, axis, [(i, (i + by) % peers) for i in range(peers)])


def product(matrix, vector):
    return jnp.dot(
        matrix, vector, precision=lax.Precision.HIGHEST, preferred_element_type=jnp.float32
    )


def face_nodes():
    i, j, k = np.meshgrid(np.arange(4), np.arange(4), np.arange(4), indexing="ij")
    node = 16 * i + 4 * j + k
    return [
        node[0].ravel(), node[3].ravel(),
        node[:, 0].ravel(), node[:, 3].ravel(),
        node[:, :, 0].ravel(), node[:, :, 3].ravel(),
    ]


def orientations():
    base = np.arange(16).reshape(4, 4)
    out = []
    for code in range(8):
        turned = base
        if code & 4:
            turned = turned.T
        if code & 1:
            turned = turned[::-1]
        if code & 2:
            turned = turned[:, ::-1]
        out.append(turned.ravel())
    return out


def selection_tables():
    nodes, perms = face_nodes(), orientations()
    pick = np.zeros((6, LANES, LANES), np.float32)
    own = np.zeros((64, 96), np.float32)
    for f in range(6):
        for code in range(8):
            for q in range(16):
                pick[f, nodes[f ^ 1][perms[code][q]], 16 * code + q] = 1.0
        for m in range(16):
            own[nodes[f][m], 16 * f + m] = 1.0
    return pick, own


def gather_kernel(idx_ref, table_ref, out_ref):
    def body(step, carry):
        for u in range(UNROLL):
            row = step * UNROLL + u
            out_ref[pl.ds(row, 1), :] = table_ref[pl.ds(idx_ref[row], 1), :]
        return carry

    lax.fori_loop(0, out_ref.shape[0] // UNROLL, body, 0)


def gather_rows(table, idx):
    return pl.pallas_call(
        gather_kernel,
        out_shape=jax.ShapeDtypeStruct((idx.shape[0], table.shape[1]), table.dtype),
        in_specs=[
            pl.BlockSpec(memory_space=pltpu.SMEM),
            pl.BlockSpec(memory_space=pltpu.VMEM),
        ],
        out_specs=pl.BlockSpec(memory_space=pltpu.VMEM),
    )(idx, table)


def split_three(x):
    high = x.astype(jnp.bfloat16)
    rest = x - high.astype(jnp.float32)
    middle = rest.astype(jnp.bfloat16)
    low = (rest - middle.astype(jnp.float32)).astype(jnp.bfloat16)
    return high, middle, low


def bf16_dot(a, b):
    return jnp.dot(a, b, preferred_element_type=jnp.float32)


def three_pass_dot(a, b):
    a_parts, b_parts = split_three(a), split_three(b)
    return bf16_dot(a_parts[0], b_parts[0]) + (
        bf16_dot(a_parts[0], b_parts[1]) + bf16_dot(a_parts[1], b_parts[0])
    )


def exact_nt_select(select, rows):
    parts = split_three(rows)
    dims = (((1,), (1,)), ((), ()))
    take = lambda part: lax.dot_general(
        select, part, dims, preferred_element_type=jnp.float32
    )
    return (take(parts[0]) + take(parts[1])) + take(parts[2])


def fused_kernel(with_send, idx_ref, send_ref, state_ref, halo_ref, mask_ref, pick_ref,
                 spread_ref, folded_ref, pick_low_ref, pick_high_ref, out_ref, *rest):
    if with_send:
        low_ref, high_ref, table, beside, sent_rows = rest
    else:
        table, beside = rest
    elements = state_ref.shape[0]
    table[0:elements, :] = state_ref[...]
    table[elements:, :] = halo_ref[...]

    def gather(step, carry):
        for u in range(UNROLL):
            row = step * UNROLL + u
            beside[pl.ds(row, 1), :] = table[pl.ds(idx_ref[row], 1), :]
        return carry

    lax.fori_loop(0, beside.shape[0] // UNROLL, gather, 0)
    state = state_ref[...]
    lifted = jnp.zeros_like(state)
    lane_code = lax.broadcasted_iota(jnp.int32, state.shape, 1) // 16
    for face in range(6):
        parts = split_three(beside[face * elements:(face + 1) * elements, :])
        turned = (bf16_dot(parts[0], pick_ref[face]) + bf16_dot(parts[1], pick_ref[face])) + (
            bf16_dot(parts[2], pick_ref[face])
        )
        chosen = jnp.where(mask_ref[face] == lane_code, turned, 0.0)
        lifted = lifted + three_pass_dot(chosen, spread_ref[face])
    own = three_pass_dot(state, folded_ref[...])
    rate = own + lifted + state - state * state * state
    out_ref[...] = state + time_step * rate
    if with_send:
        def send(step, carry):
            for u in range(UNROLL):
                row = step * UNROLL + u
                sent_rows[pl.ds(row, 1), :] = out_ref[pl.ds(send_ref[row], 1), :]
            return carry

        lax.fori_loop(0, sent_rows.shape[0] // UNROLL, send, 0)
        half = sent_rows.shape[0] // 2
        low_ref[...] = exact_nt_select(pick_low_ref[...], sent_rows[0:half, :])
        high_ref[...] = exact_nt_select(pick_high_ref[...], sent_rows[half:, :])


def fused_step(state, halo, mask, pick, spread, folded, nbr_rows, send_rows, with_send):
    elements, lanes = state.shape
    block = jax.ShapeDtypeStruct((elements, lanes), state.dtype)
    shapes = [block]
    scratch = [
        pltpu.VMEM((elements + halo.shape[0], lanes), jnp.float32),
        pltpu.VMEM((nbr_rows.shape[0], lanes), jnp.float32),
    ]
    if with_send:
        trace = jax.ShapeDtypeStruct((16, send_rows.shape[0] // 2), state.dtype)
        shapes += [trace, trace]
        scratch.append(pltpu.VMEM((send_rows.shape[0], lanes), jnp.float32))
    lane = jnp.arange(lanes)[None, :]
    spot = jnp.arange(16)[:, None]
    pick_low = (lane == spot).astype(jnp.bfloat16)
    pick_high = (lane == spot + 48).astype(jnp.bfloat16)
    vmem = pl.BlockSpec(memory_space=pltpu.VMEM)
    smem = pl.BlockSpec(memory_space=pltpu.SMEM)
    flops = 2 * 6 * 6 * elements * lanes * (2 * lanes) + 2 * 6 * elements * lanes * lanes
    moved = 4 * (4 * elements * lanes + mask.size + pick.size + spread.size)
    result = pl.pallas_call(
        functools.partial(fused_kernel, with_send),
        out_shape=tuple(shapes),
        in_specs=[smem, smem] + [vmem] * 8,
        out_specs=tuple([vmem] * len(shapes)),
        scratch_shapes=scratch,
        cost_estimate=pl.CostEstimate(flops=flops, transcendentals=0, bytes_accessed=moved),
    )(nbr_rows, send_rows, state, halo, mask, pick, spread, folded, pick_low, pick_high)
    return result


def shards(start_state, stiffness, lifting, coarse, neighbor, orientation, send_low, send_high):
    pick_np, own_np = selection_tables()
    pick = jnp.asarray(pick_np, dtype=jnp.bfloat16)
    own = jnp.asarray(own_np)
    lift_t = lifting.T.reshape(6, 16, 64)
    spread = jnp.broadcast_to(lift_t[:, None], (6, 8, 16, 64)).reshape(6, LANES, 64)
    folded = stiffness.T - product(own, lifting.T)
    mask = orientation[:, :, None]
    nbr_rows = neighbor.reshape(-1)
    send_rows = jnp.concatenate([send_low, send_high])
    spread = jnp.pad(spread, ((0, 0), (0, 0), (0, LANES - 64)))
    folded = jnp.pad(folded, ((0, LANES - 64), (0, LANES - 64)))

    state_start = start_state[0]
    state = jnp.pad(state_start.T, ((0, 0), (0, LANES - state_start.shape[0])))
    sent = gather_rows(state, send_rows)
    half = send_low.shape[0]
    low_trace, high_trace = sent[:half, 0:16].T, sent[half:, 48:64].T
    for step_id in range(STEPS):
        before = ring(high_trace, "space", 1)
        after = ring(low_trace, "space", -1)
        halo = jnp.concatenate(
            [
                jnp.pad(before.T, ((0, 0), (48, LANES - 64))),
                jnp.pad(after.T, ((0, 0), (0, LANES - 16))),
            ],
            axis=0,
        )
        with_send = step_id < STEPS - 1
        result = fused_step(
            state, halo, mask, pick, spread, folded, nbr_rows, send_rows, with_send
        )
        state = result[0]
        if with_send:
            low_trace, high_trace = result[1], result[2]
    fine_state = state[:, : state_start.shape[0]].T
    coarse_start = product(coarse, state_start)
    defect = fine_state - coarse_start
    is_first = lax.axis_index("tm") == 0
    total = jnp.where(is_first, coarse_start + defect, defect)
    return scan_over_time(total, coarse)[None]


def scan_over_time(total, coarse):
    peers = lax.axis_size("tm")
    core = lax.axis_index("tm") % 2
    partner = [(i, i ^ 1) for i in range(peers)]
    half = total.shape[1] // 2
    low, high = total[:, :half], total[:, half:]
    got = lax.ppermute(jnp.where(core == 0, high, low), "tm", partner)
    keep = jnp.where(core == 0, low, high)
    first = jnp.where(core == 0, keep, got)
    second = jnp.where(core == 0, got, keep)
    aggregate = product(coarse, first) + second
    square = product(coarse, coarse)
    before = from_behind(aggregate, "tm", 2)
    power = square
    shift = 1
    while shift < peers // 2:
        before = before + product(power, from_behind(before, "tm", 2 * shift))
        shift *= 2
        if shift < peers // 2:
            power = product(power, power)
    end_first = product(coarse, before) + first
    end_second = product(square, before) + aggregate
    mine = jnp.where(core == 0, end_first, end_second)
    got = lax.ppermute(jnp.where(core == 0, end_second, end_first), "tm", partner)
    return jnp.where(
        core == 0,
        jnp.concatenate([mine, got], axis=1),
        jnp.concatenate([got, mine], axis=1),
    )


def solution(mesh):
    return jax.shard_map(
        shards,
        mesh=mesh,
        in_specs=(
            P("tm", None, "space"),
            P(),
            P(),
            P(),
            P(None, "space"),
            P(None, "space"),
            P("space"),
            P("space"),
        ),
        out_specs=P("tm", None, "space"),
        check_vma=False,
    )
```

```python
import functools

import numpy as np
import jax
import jax.numpy as jnp
from jax import lax
from jax.experimental import pallas as pl
from jax.experimental.pallas import tpu as pltpu
from jax.sharding import PartitionSpec as P

STEPS = 3
LANES = 128
UNROLL = 256


time_step = 0.05


def from_behind(shard, axis, by):
    peers = lax.axis_size(axis)
    pairs = [(i, i + by) for i in range(peers) if 0 <= i + by < peers]
    return lax.ppermute(shard, axis, pairs)


def ring(shard, axis, by):
    peers = lax.axis_size(axis)
    return lax.ppermute(shard, axis, [(i, (i + by) % peers) for i in range(peers)])


def product(matrix, vector):
    return jnp.dot(
        matrix, vector, precision=lax.Precision.HIGHEST, preferred_element_type=jnp.float32
    )


def face_nodes():
    i, j, k = np.meshgrid(np.arange(4), np.arange(4), np.arange(4), indexing="ij")
    node = 16 * i + 4 * j + k
    return [
        node[0].ravel(), node[3].ravel(),
        node[:, 0].ravel(), node[:, 3].ravel(),
        node[:, :, 0].ravel(), node[:, :, 3].ravel(),
    ]


def orientations():
    base = np.arange(16).reshape(4, 4)
    out = []
    for code in range(8):
        turned = base
        if code & 4:
            turned = turned.T
        if code & 1:
            turned = turned[::-1]
        if code & 2:
            turned = turned[:, ::-1]
        out.append(turned.ravel())
    return out


def selection_tables():
    nodes, perms = face_nodes(), orientations()
    pick = np.zeros((6, LANES, LANES), np.float32)
    own = np.zeros((64, 96), np.float32)
    for f in range(6):
        for code in range(8):
            for q in range(16):
                pick[f, nodes[f ^ 1][perms[code][q]], 16 * code + q] = 1.0
        for m in range(16):
            own[nodes[f][m], 16 * f + m] = 1.0
    return pick, own


def gather_kernel(*refs):
    table_ref, out_ref = refs[-2:]
    start = 0
    for idx_ref in refs[:-2]:
        def body(step, carry, idx_ref=idx_ref, start=start):
            for u in range(UNROLL):
                row = step * UNROLL + u
                out_ref[pl.ds(start + row, 1), :] = table_ref[pl.ds(idx_ref[row], 1), :]
            return carry

        lax.fori_loop(0, idx_ref.shape[0] // UNROLL, body, 0)
        start += idx_ref.shape[0]


def gather_rows(table, *idx):
    return pl.pallas_call(
        gather_kernel,
        out_shape=jax.ShapeDtypeStruct((sum(part.shape[0] for part in idx), table.shape[1]), table.dtype),
        in_specs=[
            *[pl.BlockSpec(memory_space=pltpu.SMEM)] * len(idx),
            pl.BlockSpec(memory_space=pltpu.VMEM),
        ],
        out_specs=pl.BlockSpec(memory_space=pltpu.VMEM),
    )(*idx, table)


def split_three(x):
    high = x.astype(jnp.bfloat16)
    rest = x - high.astype(jnp.float32)
    middle = rest.astype(jnp.bfloat16)
    low = (rest - middle.astype(jnp.float32)).astype(jnp.bfloat16)
    return high, middle, low


def bf16_dot(a, b):
    return jnp.dot(a, b, preferred_element_type=jnp.float32)


def three_pass_dot(a, b):
    a_parts, b_parts = split_three(a), split_three(b)
    return bf16_dot(a_parts[0], b_parts[0]) + (
        bf16_dot(a_parts[0], b_parts[1]) + bf16_dot(a_parts[1], b_parts[0])
    )


def fused_kernel(with_send, idx_ref, send_low_ref, send_high_ref, state_ref, halo_ref, mask_ref, pick_ref,
                 spread_ref, folded_ref, out_ref, *rest):
    if with_send:
        sent_ref, table, beside = rest
    else:
        table, beside = rest
    elements = state_ref.shape[0]
    table[0:elements, :] = state_ref[...]
    table[elements:, :] = halo_ref[...]

    def gather(step, carry):
        for u in range(UNROLL):
            row = step * UNROLL + u
            beside[pl.ds(row, 1), :] = table[pl.ds(idx_ref[row], 1), :]
        return carry

    lax.fori_loop(0, beside.shape[0] // UNROLL, gather, 0)
    state = state_ref[...]
    lifted = jnp.zeros_like(state)
    lane_code = lax.broadcasted_iota(jnp.int32, state.shape, 1) // 16
    for face in range(6):
        parts = split_three(beside[face * elements:(face + 1) * elements, :])
        turned = (bf16_dot(parts[0], pick_ref[face]) + bf16_dot(parts[1], pick_ref[face])) + (
            bf16_dot(parts[2], pick_ref[face])
        )
        chosen = jnp.where(mask_ref[face] == lane_code, turned, 0.0)
        lifted = lifted + three_pass_dot(chosen, spread_ref[face])
    own = three_pass_dot(state, folded_ref[...])
    rate = own + lifted + state - state * state * state
    out_ref[...] = state + time_step * rate
    if with_send:
        start = 0
        for send_ref in (send_low_ref, send_high_ref):
            def send(step, carry, send_ref=send_ref, start=start):
                for u in range(UNROLL):
                    row = step * UNROLL + u
                    sent_ref[pl.ds(start + row, 1), :] = out_ref[pl.ds(send_ref[row], 1), :]
                return carry

            lax.fori_loop(0, send_ref.shape[0] // UNROLL, send, 0)
            start += send_ref.shape[0]


def fused_step(state, halo, mask, pick, spread, folded, nbr_rows, send_low, send_high,
               with_send):
    elements, lanes = state.shape
    block = jax.ShapeDtypeStruct((elements, lanes), state.dtype)
    shapes = [block]
    if with_send:
        rows = send_low.shape[0] + send_high.shape[0]
        shapes.append(jax.ShapeDtypeStruct((rows, lanes), state.dtype))
    vmem = pl.BlockSpec(memory_space=pltpu.VMEM)
    smem = pl.BlockSpec(memory_space=pltpu.SMEM)
    flops = 2 * 6 * 6 * elements * lanes * (2 * lanes) + 2 * 6 * elements * lanes * lanes
    moved = 4 * (4 * elements * lanes + mask.size + pick.size + spread.size)
    result = pl.pallas_call(
        functools.partial(fused_kernel, with_send),
        out_shape=tuple(shapes),
        in_specs=[smem, smem, smem] + [vmem] * 6,
        out_specs=tuple([vmem] * len(shapes)),
        scratch_shapes=[
            pltpu.VMEM((elements + halo.shape[0], lanes), jnp.float32),
            pltpu.VMEM((nbr_rows.shape[0], lanes), jnp.float32),
        ],
        cost_estimate=pl.CostEstimate(flops=flops, transcendentals=0, bytes_accessed=moved),
    )(nbr_rows, send_low, send_high, state, halo, mask, pick, spread, folded)
    return result


def shards(start_state, stiffness, lifting, coarse, neighbor, orientation, send_low, send_high):
    pick_np, own_np = selection_tables()
    pick = jnp.asarray(pick_np, dtype=jnp.bfloat16)
    own = jnp.asarray(own_np)
    lift_t = lifting.T.reshape(6, 16, 64)
    spread = jnp.broadcast_to(lift_t[:, None], (6, 8, 16, 64)).reshape(6, LANES, 64)
    folded = stiffness.T - product(own, lifting.T)
    mask = orientation[:, :, None]
    nbr_rows = neighbor.reshape(-1)
    spread = jnp.pad(spread, ((0, 0), (0, 0), (0, LANES - 64)))
    folded = jnp.pad(folded, ((0, LANES - 64), (0, LANES - 64)))

    state_start = start_state[0]
    state = jnp.pad(state_start.T, ((0, 0), (0, LANES - state_start.shape[0])))
    sent = gather_rows(state, send_low, send_high)
    half = send_low.shape[0]
    for step_id in range(STEPS):
        before = ring(sent[half:, 48:64].T, "space", 1)
        after = ring(sent[:half, 0:16].T, "space", -1)
        halo = jnp.concatenate(
            [
                jnp.pad(before.T, ((0, 0), (48, LANES - 64))),
                jnp.pad(after.T, ((0, 0), (0, LANES - 16))),
            ],
            axis=0,
        )
        with_send = step_id < STEPS - 1
        result = fused_step(
            state, halo, mask, pick, spread, folded, nbr_rows, send_low, send_high, with_send
        )
        state = result[0]
        if with_send:
            sent = result[1]
    fine_state = state[:, : state_start.shape[0]].T
    coarse_start = product(coarse, state_start)
    defect = fine_state - coarse_start
    is_first = lax.axis_index("tm") == 0
    total = jnp.where(is_first, coarse_start + defect, defect)
    return scan_over_time(total, coarse)[None]


def scan_over_time(total, coarse):
    peers = lax.axis_size("tm")
    core = lax.axis_index("tm") % 2
    partner = [(i, i ^ 1) for i in range(peers)]
    half = total.shape[1] // 2
    low, high = total[:, :half], total[:, half:]
    got = lax.ppermute(jnp.where(core == 0, high, low), "tm", partner)
    keep = jnp.where(core == 0, low, high)
    first = jnp.where(core == 0, keep, got)
    second = jnp.where(core == 0, got, keep)
    aggregate = product(coarse, first) + second
    square = product(coarse, coarse)
    before = from_behind(aggregate, "tm", 2)
    power = square
    shift = 1
    while shift < peers // 2:
        before = before + product(power, from_behind(before, "tm", 2 * shift))
        shift *= 2
        if shift < peers // 2:
            power = product(power, power)
    end_first = product(coarse, before) + first
    end_second = product(square, before) + aggregate
    mine = jnp.where(core == 0, end_first, end_second)
    got = lax.ppermute(jnp.where(core == 0, end_second, end_first), "tm", partner)
    return jnp.where(
        core == 0,
        jnp.concatenate([mine, got], axis=1),
        jnp.concatenate([got, mine], axis=1),
    )


def solution(mesh):
    return jax.shard_map(
        shards,
        mesh=mesh,
        in_specs=(
            P("tm", None, "space"),
            P(),
            P(),
            P(),
            P(None, "space"),
            P(None, "space"),
            P("space"),
            P("space"),
        ),
        out_specs=P("tm", None, "space"),
        check_vma=False,
    )
```

```python
import functools

import numpy as np
import jax
import jax.numpy as jnp
from jax import lax
from jax.experimental import pallas as pl
from jax.experimental.pallas import tpu as pltpu
from jax.sharding import PartitionSpec as P

STEPS = 3
LANES = 128
UNROLL = 256


time_step = 0.05


def from_behind(shard, axis, by):
    peers = lax.axis_size(axis)
    pairs = [(i, i + by) for i in range(peers) if 0 <= i + by < peers]
    return lax.ppermute(shard, axis, pairs)


def ring(shard, axis, by):
    peers = lax.axis_size(axis)
    return lax.ppermute(shard, axis, [(i, (i + by) % peers) for i in range(peers)])


def product(matrix, vector):
    return jnp.dot(
        matrix, vector, precision=lax.Precision.HIGHEST, preferred_element_type=jnp.float32
    )


def face_nodes():
    i, j, k = np.meshgrid(np.arange(4), np.arange(4), np.arange(4), indexing="ij")
    node = 16 * i + 4 * j + k
    return [
        node[0].ravel(), node[3].ravel(),
        node[:, 0].ravel(), node[:, 3].ravel(),
        node[:, :, 0].ravel(), node[:, :, 3].ravel(),
    ]


def orientations():
    base = np.arange(16).reshape(4, 4)
    out = []
    for code in range(8):
        turned = base
        if code & 4:
            turned = turned.T
        if code & 1:
            turned = turned[::-1]
        if code & 2:
            turned = turned[:, ::-1]
        out.append(turned.ravel())
    return out


def selection_tables():
    nodes, perms = face_nodes(), orientations()
    pick = np.zeros((6, LANES, LANES), np.float32)
    own = np.zeros((64, 96), np.float32)
    for f in range(6):
        for code in range(8):
            for q in range(16):
                pick[f, nodes[f ^ 1][perms[code][q]], 16 * code + q] = 1.0
        for m in range(16):
            own[nodes[f][m], 16 * f + m] = 1.0
    return pick, own


def gather_kernel(*refs):
    table_ref, out_ref = refs[-2:]
    start = 0
    for idx_ref in refs[:-2]:
        def body(step, carry, idx_ref=idx_ref, start=start):
            for u in range(UNROLL):
                row = step * UNROLL + u
                out_ref[pl.ds(start + row, 1), :] = table_ref[pl.ds(idx_ref[row], 1), :]
            return carry

        lax.fori_loop(0, idx_ref.shape[0] // UNROLL, body, 0)
        start += idx_ref.shape[0]


def gather_rows(table, *idx):
    return pl.pallas_call(
        gather_kernel,
        out_shape=jax.ShapeDtypeStruct((sum(part.shape[0] for part in idx), table.shape[1]), table.dtype),
        in_specs=[
            *[pl.BlockSpec(memory_space=pltpu.SMEM)] * len(idx),
            pl.BlockSpec(memory_space=pltpu.VMEM),
        ],
        out_specs=pl.BlockSpec(memory_space=pltpu.VMEM),
    )(*idx, table)


def split_three(x):
    high = x.astype(jnp.bfloat16)
    rest = x - high.astype(jnp.float32)
    middle = rest.astype(jnp.bfloat16)
    low = (rest - middle.astype(jnp.float32)).astype(jnp.bfloat16)
    return high, middle, low


def bf16_dot(a, b):
    return jnp.dot(a, b, preferred_element_type=jnp.float32)


def three_pass_dot(a, b):
    a_parts, b_parts = split_three(a), split_three(b)
    return bf16_dot(a_parts[0], b_parts[0]) + (
        bf16_dot(a_parts[0], b_parts[1]) + bf16_dot(a_parts[1], b_parts[0])
    )


def fused_kernel(with_send, idx_ref, send_low_ref, send_high_ref, state_ref, halo_ref, mask_ref, pick_ref,
                 spread_ref, folded_ref, out_ref, *rest):
    if with_send:
        sent_ref, table, beside = rest
    else:
        table, beside = rest
    elements = state_ref.shape[0]
    table[0:elements, :] = state_ref[...]
    table[elements:, :] = halo_ref[...]

    def gather(step, carry):
        for u in range(UNROLL):
            row = step * UNROLL + u
            beside[pl.ds(row, 1), :] = table[pl.ds(idx_ref[row], 1), :]
        return carry

    lax.fori_loop(0, beside.shape[0] // UNROLL, gather, 0)
    state = state_ref[...]
    lifted = jnp.zeros_like(state)
    lane_code = lax.broadcasted_iota(jnp.int32, state.shape, 1) // 16
    for face in range(6):
        parts = split_three(beside[face * elements:(face + 1) * elements, :])
        turned = (bf16_dot(parts[0], pick_ref[face]) + bf16_dot(parts[1], pick_ref[face])) + (
            bf16_dot(parts[2], pick_ref[face])
        )
        chosen = jnp.where(mask_ref[face] == lane_code, turned, 0.0)
        lifted = lifted + three_pass_dot(chosen, spread_ref[face])
    own = three_pass_dot(state, folded_ref[...])
    rate = own + lifted + state - state * state * state
    out_ref[...] = state + time_step * rate
    if with_send:
        start = 0
        for send_ref in (send_low_ref, send_high_ref):
            def send(step, carry, send_ref=send_ref, start=start):
                for u in range(UNROLL):
                    row = step * UNROLL + u
                    sent_ref[pl.ds(start + row, 1), :] = out_ref[pl.ds(send_ref[row], 1), :]
                return carry

            lax.fori_loop(0, send_ref.shape[0] // UNROLL, send, 0)
            start += send_ref.shape[0]


def fused_step(state, halo, mask, pick, spread, folded, nbr_rows, send_low, send_high,
               with_send):
    elements, lanes = state.shape
    block = jax.ShapeDtypeStruct((elements, lanes), state.dtype)
    shapes = [block]
    if with_send:
        rows = send_low.shape[0] + send_high.shape[0]
        shapes.append(jax.ShapeDtypeStruct((rows, lanes), state.dtype))
    vmem = pl.BlockSpec(memory_space=pltpu.VMEM)
    smem = pl.BlockSpec(memory_space=pltpu.SMEM)
    flops = 2 * 6 * 6 * elements * lanes * (2 * lanes) + 2 * 6 * elements * lanes * lanes
    moved = 4 * (4 * elements * lanes + mask.size + pick.size + spread.size)
    result = pl.pallas_call(
        functools.partial(fused_kernel, with_send),
        out_shape=tuple(shapes),
        in_specs=[smem, smem, smem] + [vmem] * 6,
        out_specs=tuple([vmem] * len(shapes)),
        scratch_shapes=[
            pltpu.VMEM((elements + halo.shape[0], lanes), jnp.float32),
            pltpu.VMEM((nbr_rows.shape[0], lanes), jnp.float32),
        ],
        cost_estimate=pl.CostEstimate(flops=flops, transcendentals=0, bytes_accessed=moved),
    )(nbr_rows, send_low, send_high, state, halo, mask, pick, spread, folded)
    return result


def shards(start_state, stiffness, lifting, coarse, neighbor, orientation, send_low, send_high):
    pick_np, own_np = selection_tables()
    pick = jnp.asarray(pick_np, dtype=jnp.bfloat16)
    own = jnp.asarray(own_np)
    lift_t = lifting.T.reshape(6, 16, 64)
    spread = jnp.broadcast_to(lift_t[:, None], (6, 8, 16, 64)).reshape(6, LANES, 64)
    folded = stiffness.T - product(own, lifting.T)
    mask = orientation[:, :, None]
    nbr_rows = neighbor.reshape(-1)
    spread = jnp.pad(spread, ((0, 0), (0, 0), (0, LANES - 64)))
    folded = jnp.pad(folded, ((0, LANES - 64), (0, LANES - 64)))

    state_start = start_state[0]
    state = jnp.pad(state_start.T, ((0, 0), (0, LANES - state_start.shape[0])))
    sent = gather_rows(state, send_low, send_high)
    half = send_low.shape[0]
    for step_id in range(STEPS):
        before = ring(sent[half:, 48:64].T, "space", 1)
        after = ring(sent[:half, 0:16].T, "space", -1)
        halo = jnp.concatenate(
            [
                jnp.pad(before.T, ((0, 0), (48, LANES - 64))),
                jnp.pad(after.T, ((0, 0), (0, LANES - 16))),
            ],
            axis=0,
        )
        with_send = step_id < STEPS - 1
        result = fused_step(
            state, halo, mask, pick, spread, folded, nbr_rows, send_low, send_high, with_send
        )
        state = result[0]
        if with_send:
            sent = result[1]
    fine_state = state[:, : state_start.shape[0]].T
    coarse_start = product(coarse, state_start)
    defect = fine_state - coarse_start
    is_first = lax.axis_index("tm") == 0
    total = jnp.where(is_first, coarse_start + defect, defect)
    return scan_over_time(total, coarse)[None]


def scan_over_time(total, coarse):
    peers = lax.axis_size("tm")
    core = lax.axis_index("tm") % 2
    partner = [(i, i ^ 1) for i in range(peers)]
    half = total.shape[1] // 2
    keep = lax.dynamic_slice_in_dim(total, core * half, half, axis=1)
    got = lax.ppermute(
        lax.dynamic_slice_in_dim(total, (1 - core) * half, half, axis=1), "tm", partner
    )
    first = jnp.where(core == 0, keep, got)
    second = jnp.where(core == 0, got, keep)
    aggregate = product(coarse, first) + second
    square = product(coarse, coarse)
    before = from_behind(aggregate, "tm", 2)
    power = square
    shift = 1
    while shift < peers // 2:
        before = before + product(power, from_behind(before, "tm", 2 * shift))
        shift *= 2
        if shift < peers // 2:
            power = product(power, power)
    end_first = product(coarse, before) + first
    end_second = product(square, before) + aggregate
    mine = jnp.where(core == 0, end_first, end_second)
    got = lax.ppermute(jnp.where(core == 0, end_second, end_first), "tm", partner)
    whole = jnp.concatenate([got, got], axis=1)
    return lax.dynamic_update_slice_in_dim(whole, mine, core * half, axis=1)


def solution(mesh):
    return jax.shard_map(
        shards,
        mesh=mesh,
        in_specs=(
            P("tm", None, "space"),
            P(),
            P(),
            P(),
            P(None, "space"),
            P(None, "space"),
            P("space"),
            P("space"),
        ),
        out_specs=P("tm", None, "space"),
        check_vma=False,
    )
```

```python
import functools

import numpy as np
import jax
import jax.numpy as jnp
from jax import lax
from jax.experimental import pallas as pl
from jax.experimental.pallas import tpu as pltpu
from jax.sharding import PartitionSpec as P

STEPS = 3
LANES = 128
UNROLL = 256


time_step = 0.05


def from_behind(shard, axis, by):
    peers = lax.axis_size(axis)
    pairs = [(i, i + by) for i in range(peers) if 0 <= i + by < peers]
    return lax.ppermute(shard, axis, pairs)


def ring(shard, axis, by):
    peers = lax.axis_size(axis)
    return lax.ppermute(shard, axis, [(i, (i + by) % peers) for i in range(peers)])


def product(matrix, vector):
    return jnp.dot(
        matrix, vector, precision=lax.Precision.HIGHEST, preferred_element_type=jnp.float32
    )


def face_nodes():
    i, j, k = np.meshgrid(np.arange(4), np.arange(4), np.arange(4), indexing="ij")
    node = 16 * i + 4 * j + k
    return [
        node[0].ravel(), node[3].ravel(),
        node[:, 0].ravel(), node[:, 3].ravel(),
        node[:, :, 0].ravel(), node[:, :, 3].ravel(),
    ]


def orientations():
    base = np.arange(16).reshape(4, 4)
    out = []
    for code in range(8):
        turned = base
        if code & 4:
            turned = turned.T
        if code & 1:
            turned = turned[::-1]
        if code & 2:
            turned = turned[:, ::-1]
        out.append(turned.ravel())
    return out


def selection_tables():
    nodes, perms = face_nodes(), orientations()
    pick = np.zeros((6, LANES, LANES), np.float32)
    own = np.zeros((64, 96), np.float32)
    for f in range(6):
        for code in range(8):
            for q in range(16):
                pick[f, nodes[f ^ 1][perms[code][q]], 16 * code + q] = 1.0
        for m in range(16):
            own[nodes[f][m], 16 * f + m] = 1.0
    return pick, own


def gather_kernel(*refs):
    table_ref, out_ref = refs[-2:]
    start = 0
    for idx_ref in refs[:-2]:
        def body(step, carry, idx_ref=idx_ref, start=start):
            for u in range(UNROLL):
                row = step * UNROLL + u
                out_ref[pl.ds(start + row, 1), :] = table_ref[pl.ds(idx_ref[row], 1), :]
            return carry

        lax.fori_loop(0, idx_ref.shape[0] // UNROLL, body, 0)
        start += idx_ref.shape[0]


def gather_rows(table, *idx):
    return pl.pallas_call(
        gather_kernel,
        out_shape=jax.ShapeDtypeStruct((sum(part.shape[0] for part in idx), table.shape[1]), table.dtype),
        in_specs=[
            *[pl.BlockSpec(memory_space=pltpu.SMEM)] * len(idx),
            pl.BlockSpec(memory_space=pltpu.VMEM),
        ],
        out_specs=pl.BlockSpec(memory_space=pltpu.VMEM),
    )(*idx, table)


def split_three(x):
    high = x.astype(jnp.bfloat16)
    rest = x - high.astype(jnp.float32)
    middle = rest.astype(jnp.bfloat16)
    low = (rest - middle.astype(jnp.float32)).astype(jnp.bfloat16)
    return high, middle, low


def bf16_dot(a, b):
    return jnp.dot(a, b, preferred_element_type=jnp.float32)


def three_pass_dot(a, b):
    a_parts, b_parts = split_three(a), split_three(b)
    return bf16_dot(a_parts[0], b_parts[0]) + (
        bf16_dot(a_parts[0], b_parts[1]) + bf16_dot(a_parts[1], b_parts[0])
    )


def fused_kernel(with_send, idx_ref, send_low_ref, send_high_ref, state_ref, low_halo_ref,
                 high_halo_ref, mask_ref, pick_ref,
                 spread_ref, folded_ref, out_ref, *rest):
    if with_send:
        sent_ref, table, beside = rest
    else:
        table, beside = rest
    elements = state_ref.shape[0]
    table[0:elements, :] = state_ref[...]
    table[elements:, :] = jnp.zeros((table.shape[0] - elements, table.shape[1]), jnp.float32)
    rows = low_halo_ref.shape[0]
    table[elements:elements + rows, 48:64] = low_halo_ref[...]
    table[elements + rows:, 0:16] = high_halo_ref[...]

    def gather(step, carry):
        for u in range(UNROLL):
            row = step * UNROLL + u
            beside[pl.ds(row, 1), :] = table[pl.ds(idx_ref[row], 1), :]
        return carry

    lax.fori_loop(0, beside.shape[0] // UNROLL, gather, 0)
    state = state_ref[...]
    lifted = jnp.zeros_like(state)
    lane_code = lax.broadcasted_iota(jnp.int32, state.shape, 1) // 16
    for face in range(6):
        parts = split_three(beside[face * elements:(face + 1) * elements, :])
        turned = (bf16_dot(parts[0], pick_ref[face]) + bf16_dot(parts[1], pick_ref[face])) + (
            bf16_dot(parts[2], pick_ref[face])
        )
        chosen = jnp.where(mask_ref[face] == lane_code, turned, 0.0)
        lifted = lifted + three_pass_dot(chosen, spread_ref[face])
    own = three_pass_dot(state, folded_ref[...])
    rate = own + lifted + state - state * state * state
    out_ref[...] = state + time_step * rate
    if with_send:
        start = 0
        for send_ref in (send_low_ref, send_high_ref):
            def send(step, carry, send_ref=send_ref, start=start):
                for u in range(UNROLL):
                    row = step * UNROLL + u
                    sent_ref[pl.ds(start + row, 1), :] = out_ref[pl.ds(send_ref[row], 1), :]
                return carry

            lax.fori_loop(0, send_ref.shape[0] // UNROLL, send, 0)
            start += send_ref.shape[0]


def fused_step(state, halo, mask, pick, spread, folded, nbr_rows, send_low, send_high,
               with_send):
    elements, lanes = state.shape
    block = jax.ShapeDtypeStruct((elements, lanes), state.dtype)
    shapes = [block]
    if with_send:
        rows = send_low.shape[0] + send_high.shape[0]
        shapes.append(jax.ShapeDtypeStruct((rows, lanes), state.dtype))
    vmem = pl.BlockSpec(memory_space=pltpu.VMEM)
    smem = pl.BlockSpec(memory_space=pltpu.SMEM)
    flops = 2 * 6 * 6 * elements * lanes * (2 * lanes) + 2 * 6 * elements * lanes * lanes
    moved = 4 * (4 * elements * lanes + mask.size + pick.size + spread.size)
    result = pl.pallas_call(
        functools.partial(fused_kernel, with_send),
        out_shape=tuple(shapes),
        in_specs=[smem, smem, smem] + [vmem] * 7,
        out_specs=tuple([vmem] * len(shapes)),
        scratch_shapes=[
            pltpu.VMEM((elements + 2 * halo[0].shape[0], lanes), jnp.float32),
            pltpu.VMEM((nbr_rows.shape[0], lanes), jnp.float32),
        ],
        cost_estimate=pl.CostEstimate(flops=flops, transcendentals=0, bytes_accessed=moved),
    )(nbr_rows, send_low, send_high, state, halo[0], halo[1], mask, pick, spread, folded)
    return result


def shards(start_state, stiffness, lifting, coarse, neighbor, orientation, send_low, send_high):
    pick_np, own_np = selection_tables()
    pick = jnp.asarray(pick_np, dtype=jnp.bfloat16)
    own = jnp.asarray(own_np)
    lift_t = lifting.T.reshape(6, 16, 64)
    spread = jnp.broadcast_to(lift_t[:, None], (6, 8, 16, 64)).reshape(6, LANES, 64)
    folded = stiffness.T - product(own, lifting.T)
    mask = orientation[:, :, None]
    nbr_rows = neighbor.reshape(-1)
    spread = jnp.pad(spread, ((0, 0), (0, 0), (0, LANES - 64)))
    folded = jnp.pad(folded, ((0, LANES - 64), (0, LANES - 64)))

    state_start = start_state[0]
    state = jnp.pad(state_start.T, ((0, 0), (0, LANES - state_start.shape[0])))
    sent = gather_rows(state, send_low, send_high)
    half = send_low.shape[0]
    for step_id in range(STEPS):
        before = ring(sent[half:, 48:64].T, "space", 1)
        after = ring(sent[:half, 0:16].T, "space", -1)
        halo = (before.T, after.T)
        with_send = step_id < STEPS - 1
        result = fused_step(
            state, halo, mask, pick, spread, folded, nbr_rows, send_low, send_high, with_send
        )
        state = result[0]
        if with_send:
            sent = result[1]
    fine_state = state[:, : state_start.shape[0]].T
    coarse_start = product(coarse, state_start)
    defect = fine_state - coarse_start
    is_first = lax.axis_index("tm") == 0
    total = jnp.where(is_first, coarse_start + defect, defect)
    return scan_over_time(total, coarse)[None]


def scan_over_time(total, coarse):
    peers = lax.axis_size("tm")
    core = lax.axis_index("tm") % 2
    partner = [(i, i ^ 1) for i in range(peers)]
    half = total.shape[1] // 2
    low, high = total[:, :half], total[:, half:]
    got = lax.ppermute(jnp.where(core == 0, high, low), "tm", partner)
    keep = jnp.where(core == 0, low, high)
    first = jnp.where(core == 0, keep, got)
    second = jnp.where(core == 0, got, keep)
    aggregate = product(coarse, first) + second
    square = product(coarse, coarse)
    before = from_behind(aggregate, "tm", 2)
    power = square
    shift = 1
    while shift < peers // 2:
        before = before + product(power, from_behind(before, "tm", 2 * shift))
        shift *= 2
        if shift < peers // 2:
            power = product(power, power)
    end_first = product(coarse, before) + first
    end_second = product(square, before) + aggregate
    mine = jnp.where(core == 0, end_first, end_second)
    got = lax.ppermute(jnp.where(core == 0, end_second, end_first), "tm", partner)
    return jnp.where(
        core == 0,
        jnp.concatenate([mine, got], axis=1),
        jnp.concatenate([got, mine], axis=1),
    )


def solution(mesh):
    return jax.shard_map(
        shards,
        mesh=mesh,
        in_specs=(
            P("tm", None, "space"),
            P(),
            P(),
            P(),
            P(None, "space"),
            P(None, "space"),
            P("space"),
            P("space"),
        ),
        out_specs=P("tm", None, "space"),
        check_vma=False,
    )
```

```python
import functools

import numpy as np
import jax
import jax.numpy as jnp
from jax import lax
from jax.experimental import pallas as pl
from jax.experimental.pallas import tpu as pltpu
from jax.sharding import PartitionSpec as P

STEPS = 3
LANES = 128
UNROLL = 512


time_step = 0.05


def from_behind(shard, axis, by):
    peers = lax.axis_size(axis)
    pairs = [(i, i + by) for i in range(peers) if 0 <= i + by < peers]
    return lax.ppermute(shard, axis, pairs)


def ring(shard, axis, by):
    peers = lax.axis_size(axis)
    return lax.ppermute(shard, axis, [(i, (i + by) % peers) for i in range(peers)])


def product(matrix, vector):
    return jnp.dot(
        matrix, vector, precision=lax.Precision.HIGHEST, preferred_element_type=jnp.float32
    )


def face_nodes():
    i, j, k = np.meshgrid(np.arange(4), np.arange(4), np.arange(4), indexing="ij")
    node = 16 * i + 4 * j + k
    return [
        node[0].ravel(), node[3].ravel(),
        node[:, 0].ravel(), node[:, 3].ravel(),
        node[:, :, 0].ravel(), node[:, :, 3].ravel(),
    ]


def orientations():
    base = np.arange(16).reshape(4, 4)
    out = []
    for code in range(8):
        turned = base
        if code & 4:
            turned = turned.T
        if code & 1:
            turned = turned[::-1]
        if code & 2:
            turned = turned[:, ::-1]
        out.append(turned.ravel())
    return out


def selection_tables():
    nodes, perms = face_nodes(), orientations()
    pick = np.zeros((6, LANES, LANES), np.float32)
    own = np.zeros((64, 96), np.float32)
    for f in range(6):
        for code in range(8):
            for q in range(16):
                pick[f, nodes[f ^ 1][perms[code][q]], 16 * code + q] = 1.0
        for m in range(16):
            own[nodes[f][m], 16 * f + m] = 1.0
    return pick, own


def gather_kernel(*refs):
    table_ref, out_ref = refs[-2:]
    start = 0
    for idx_ref in refs[:-2]:
        def body(step, carry, idx_ref=idx_ref, start=start):
            for u in range(UNROLL):
                row = step * UNROLL + u
                out_ref[pl.ds(start + row, 1), :] = table_ref[pl.ds(idx_ref[row], 1), :]
            return carry

        lax.fori_loop(0, idx_ref.shape[0] // UNROLL, body, 0)
        start += idx_ref.shape[0]


def gather_rows(table, *idx):
    return pl.pallas_call(
        gather_kernel,
        out_shape=jax.ShapeDtypeStruct((sum(part.shape[0] for part in idx), table.shape[1]), table.dtype),
        in_specs=[
            *[pl.BlockSpec(memory_space=pltpu.SMEM)] * len(idx),
            pl.BlockSpec(memory_space=pltpu.VMEM),
        ],
        out_specs=pl.BlockSpec(memory_space=pltpu.VMEM),
    )(*idx, table)


def split_three(x):
    high = x.astype(jnp.bfloat16)
    rest = x - high.astype(jnp.float32)
    middle = rest.astype(jnp.bfloat16)
    low = (rest - middle.astype(jnp.float32)).astype(jnp.bfloat16)
    return high, middle, low


def bf16_dot(a, b):
    return jnp.dot(a, b, preferred_element_type=jnp.float32)


def three_pass_dot(a, b):
    a_parts, b_parts = split_three(a), split_three(b)
    return bf16_dot(a_parts[0], b_parts[0]) + (
        bf16_dot(a_parts[0], b_parts[1]) + bf16_dot(a_parts[1], b_parts[0])
    )


def fused_kernel(with_send, idx_ref, send_low_ref, send_high_ref, state_ref, low_halo_ref,
                 high_halo_ref, mask_ref, pick_ref,
                 spread_ref, folded_ref, out_ref, *rest):
    if with_send:
        sent_ref, table, beside = rest
    else:
        table, beside = rest
    elements = state_ref.shape[0]
    table[0:elements, :] = state_ref[...]
    table[elements:, :] = jnp.zeros((table.shape[0] - elements, table.shape[1]), jnp.float32)
    rows = low_halo_ref.shape[0]
    table[elements:elements + rows, 48:64] = low_halo_ref[...]
    table[elements + rows:, 0:16] = high_halo_ref[...]

    def gather(step, carry):
        for u in range(UNROLL):
            row = step * UNROLL + u
            beside[pl.ds(row, 1), :] = table[pl.ds(idx_ref[row], 1), :]
        return carry

    lax.fori_loop(0, beside.shape[0] // UNROLL, gather, 0)
    state = state_ref[...]
    lifted = jnp.zeros_like(state)
    lane_code = lax.broadcasted_iota(jnp.int32, state.shape, 1) // 16
    for face in range(6):
        parts = split_three(beside[face * elements:(face + 1) * elements, :])
        turned = (bf16_dot(parts[0], pick_ref[face]) + bf16_dot(parts[1], pick_ref[face])) + (
            bf16_dot(parts[2], pick_ref[face])
        )
        chosen = jnp.where(mask_ref[face] == lane_code, turned, 0.0)
        lifted = lifted + three_pass_dot(chosen, spread_ref[face])
    own = three_pass_dot(state, folded_ref[...])
    rate = own + lifted + state - state * state * state
    out_ref[...] = state + time_step * rate
    if with_send:
        start = 0
        for send_ref in (send_low_ref, send_high_ref):
            def send(step, carry, send_ref=send_ref, start=start):
                for u in range(UNROLL):
                    row = step * UNROLL + u
                    sent_ref[pl.ds(start + row, 1), :] = out_ref[pl.ds(send_ref[row], 1), :]
                return carry

            lax.fori_loop(0, send_ref.shape[0] // UNROLL, send, 0)
            start += send_ref.shape[0]


def fused_step(state, halo, mask, pick, spread, folded, nbr_rows, send_low, send_high,
               with_send):
    elements, lanes = state.shape
    block = jax.ShapeDtypeStruct((elements, lanes), state.dtype)
    shapes = [block]
    if with_send:
        rows = send_low.shape[0] + send_high.shape[0]
        shapes.append(jax.ShapeDtypeStruct((rows, lanes), state.dtype))
    vmem = pl.BlockSpec(memory_space=pltpu.VMEM)
    smem = pl.BlockSpec(memory_space=pltpu.SMEM)
    flops = 2 * 6 * 6 * elements * lanes * (2 * lanes) + 2 * 6 * elements * lanes * lanes
    moved = 4 * (4 * elements * lanes + mask.size + pick.size + spread.size)
    result = pl.pallas_call(
        functools.partial(fused_kernel, with_send),
        out_shape=tuple(shapes),
        in_specs=[smem, smem, smem] + [vmem] * 7,
        out_specs=tuple([vmem] * len(shapes)),
        scratch_shapes=[
            pltpu.VMEM((elements + 2 * halo[0].shape[0], lanes), jnp.float32),
            pltpu.VMEM((nbr_rows.shape[0], lanes), jnp.float32),
        ],
        cost_estimate=pl.CostEstimate(flops=flops, transcendentals=0, bytes_accessed=moved),
    )(nbr_rows, send_low, send_high, state, halo[0], halo[1], mask, pick, spread, folded)
    return result


def shards(start_state, stiffness, lifting, coarse, neighbor, orientation, send_low, send_high):
    pick_np, own_np = selection_tables()
    pick = jnp.asarray(pick_np, dtype=jnp.bfloat16)
    own = jnp.asarray(own_np)
    lift_t = lifting.T.reshape(6, 16, 64)
    spread = jnp.broadcast_to(lift_t[:, None], (6, 8, 16, 64)).reshape(6, LANES, 64)
    folded = stiffness.T - product(own, lifting.T)
    mask = orientation[:, :, None]
    nbr_rows = neighbor.reshape(-1)
    spread = jnp.pad(spread, ((0, 0), (0, 0), (0, LANES - 64)))
    folded = jnp.pad(folded, ((0, LANES - 64), (0, LANES - 64)))

    state_start = start_state[0]
    state = jnp.pad(state_start.T, ((0, 0), (0, LANES - state_start.shape[0])))
    sent = gather_rows(state, send_low, send_high)
    half = send_low.shape[0]
    for step_id in range(STEPS):
        before = ring(sent[half:, 48:64].T, "space", 1)
        after = ring(sent[:half, 0:16].T, "space", -1)
        halo = (before.T, after.T)
        with_send = step_id < STEPS - 1
        result = fused_step(
            state, halo, mask, pick, spread, folded, nbr_rows, send_low, send_high, with_send
        )
        state = result[0]
        if with_send:
            sent = result[1]
    fine_state = state[:, : state_start.shape[0]].T
    coarse_start = product(coarse, state_start)
    defect = fine_state - coarse_start
    is_first = lax.axis_index("tm") == 0
    total = jnp.where(is_first, coarse_start + defect, defect)
    return scan_over_time(total, coarse)[None]


def scan_over_time(total, coarse):
    peers = lax.axis_size("tm")
    core = lax.axis_index("tm") % 2
    partner = [(i, i ^ 1) for i in range(peers)]
    half = total.shape[1] // 2
    low, high = total[:, :half], total[:, half:]
    got = lax.ppermute(jnp.where(core == 0, high, low), "tm", partner)
    keep = jnp.where(core == 0, low, high)
    first = jnp.where(core == 0, keep, got)
    second = jnp.where(core == 0, got, keep)
    aggregate = product(coarse, first) + second
    square = product(coarse, coarse)
    before = from_behind(aggregate, "tm", 2)
    power = square
    shift = 1
    while shift < peers // 2:
        before = before + product(power, from_behind(before, "tm", 2 * shift))
        shift *= 2
        if shift < peers // 2:
            power = product(power, power)
    end_first = product(coarse, before) + first
    end_second = product(square, before) + aggregate
    mine = jnp.where(core == 0, end_first, end_second)
    got = lax.ppermute(jnp.where(core == 0, end_second, end_first), "tm", partner)
    return jnp.where(
        core == 0,
        jnp.concatenate([mine, got], axis=1),
        jnp.concatenate([got, mine], axis=1),
    )


def solution(mesh):
    return jax.shard_map(
        shards,
        mesh=mesh,
        in_specs=(
            P("tm", None, "space"),
            P(),
            P(),
            P(),
            P(None, "space"),
            P(None, "space"),
            P("space"),
            P("space"),
        ),
        out_specs=P("tm", None, "space"),
        check_vma=False,
    )
```
